32 devices in a mesh: dp: 8 (over z, y), code: 4 (over x, core).
Axes of the slice: x: 2, y: 2, z: 4, core: 2. Of those that a mesh axis runs over, the one named last changes fastest.
Arguments:
- latents: bfloat16 [4096, 256], P('dp'), may hold values from -64 to 64
- codebook: bfloat16 [262144, 256], P('code'), may hold values from -1 to 1
- hard_code: int32 [4096], P('dp'), may hold values from 0 to 262143
- upstream: bfloat16 [4096, 256], P('dp'), may hold values from -12 to 12
Outputs:
- token_grad: float32 [4096, 256], P(('dp', 'code'))
- codebook_grad: float32 [262144, 256], P(('code', 'dp'))
- loss_terms: float32 [3], replicated
The draws below stay inside these ranges and needn't reach their ends.
All inputs are finite; a program needn't handle non-finite values.
Results may differ from the reference program's by a relative error of at most 0.019.
Values may be sent and summed in bfloat16 or wider, within the bound.
No kernel may reach another device: no remote copies, remote signals or barrier semaphores. Data moves between devices by JAX's collectives and lax.ppermute only.
A program may use at most 448 MiB of HBM per device.

```python
import jax
import jax.numpy as jnp
from jax import lax

D = 256
K = 262144
TOK_BLOCK = 512
TOKENS = 4096


def shared_draw(key):
    subkeys = jax.random.split(jax.random.fold_in(key, 11), 18)
    raw_table = jnp.clip(jax.random.normal(subkeys[0], (K, D), jnp.float32), -3.0, 3.0)
    code_table = (raw_table * D ** (-0.5)).astype(jnp.bfloat16)
    pool_size = TOKENS // 4
    drawn = jax.random.randint(subkeys[1], (pool_size,), 0, K)
    other = jax.random.randint(subkeys[14], (pool_size,), 0, K)
    selector = jax.random.randint(subkeys[15], (pool_size,), 0, 2)
    pool = jnp.where(selector == 0, drawn, jnp.maximum(drawn, other))
    block_of = jnp.arange(TOKENS, dtype=jnp.int32) // TOK_BLOCK
    pick = jax.random.randint(subkeys[16], (TOKENS,), 0, TOK_BLOCK // 4)
    chosen = pool[block_of * (TOK_BLOCK // 4) + pick]
    first_pos = jax.random.randint(subkeys[2], (), 0, TOKENS // 2)
    second_pos = jax.random.randint(subkeys[3], (), TOKENS // 2, TOKENS)
    chosen = chosen.at[first_pos].set(K - 1).at[second_pos].set(0)
    return (code_table, chosen, subkeys)


def draw_codebook(key, part):
    code_table, chosen, subkeys = shared_draw(key)
    return code_table


def draw_hard_code(key, part):
    code_table, chosen, subkeys = shared_draw(key)
    return chosen.astype(jnp.int32)


def draw_latents(key, part):
    code_table, chosen, subkeys = shared_draw(key)
    table = code_table.astype(jnp.float32)
    nearest = table[chosen]
    pull = jax.random.uniform(subkeys[4], (TOKENS, 1), jnp.float32, 1.6, 2.4)
    push = jax.random.uniform(subkeys[12], (TOKENS, 1), jnp.float32, 3.0, 6.0)
    opposed = jax.random.randint(subkeys[5], (TOKENS, 1), 0, 8) == 0
    jitter = jax.random.normal(subkeys[6], (TOKENS, D), jnp.float32) * 0.4
    vectors = jnp.where(opposed, -push * nearest + 0.25 * jitter, pull * nearest + jitter)
    return jnp.clip(vectors, -60.0, 60.0).astype(jnp.bfloat16)


def level_of(rng, shape, cuts, least, largest):
    loudness, own = 1.0, jax.random.fold_in(rng, 6)
    for dim, shards_of in cuts:
        heights = jnp.exp(jax.random.uniform(jax.random.fold_in(own, dim), (shards_of,), jnp.float32, least / len(cuts), largest / len(cuts)))
        loudness = loudness * jnp.repeat(heights, shape[dim] // shards_of).reshape([-1 if axis == dim else 1 for axis in range(len(shape))])
    return loudness


def centred(own_key, extent, scale, most, shards=(), held_as=jnp.bfloat16):
    factor_of = level_of(own_key, extent, shards, -0.22, 0.18) if shards else 1.0
    entries = jax.random.normal(own_key, extent, jnp.float32) * scale * factor_of
    return jnp.minimum(jnp.maximum(entries, -most), most).astype(held_as)


def setup_inputs(seed: int = 0) -> dict:
    splits = jax.random.split(jax.random.key(seed), 5)
    return {
        "latents": draw_latents(jax.random.fold_in(splits[4], 71), 0),
        "codebook": draw_codebook(jax.random.fold_in(splits[4], 71), 0),
        "hard_code": draw_hard_code(jax.random.fold_in(splits[4], 71), 0),
        "upstream": centred(splits[3], (TOKENS, D), 2.0, 12.0, ((0, 8),)),
    }


LOGIT_SCALE = 5.0
ENTROPY_WEIGHT = 0.5
usage_eps = 1e-06
norm_eps = 1e-06
cos_floor = 0.25
row_block = 128

def rotate(latent, code_vec, cotangent):
    latent_norm = jnp.sqrt(lax.optimization_barrier(jnp.sum(latent * latent, axis=1, keepdims=True)) + norm_eps)
    code_norm = jnp.sqrt(lax.optimization_barrier(jnp.sum(code_vec * code_vec, axis=1, keepdims=True)) + norm_eps)
    latent_dir = latent / latent_norm
    code_dir = code_vec / code_norm
    cosine = lax.optimization_barrier(jnp.sum(latent_dir * code_dir, axis=1, keepdims=True))
    summed = latent_dir + code_dir
    along = lax.optimization_barrier(jnp.sum(summed * cotangent, axis=1, keepdims=True))
    facing = lax.optimization_barrier(jnp.sum(code_dir * cotangent, axis=1, keepdims=True))
    turned = cotangent - summed * along / jnp.maximum(1.0 + cosine, cos_floor) + 2.0 * latent_dir * facing
    return code_norm / latent_norm * turned

def reference(latents, codebook, hard_code, upstream):
    tokens_total = latents.shape[0]
    code_total = codebook.shape[0]
    width = latents.shape[1]
    block_lat = latents.reshape(tokens_total // row_block, row_block, width)
    block_hard = hard_code.reshape(tokens_total // row_block, row_block)
    block_up = upstream.reshape(tokens_total // row_block, row_block, width)

    def scores(block_rows):
        return LOGIT_SCALE * lax.dot_general(block_rows, codebook, (((1,), (1,)), ((), ())), preferred_element_type=jnp.float32)

    def first_pass(usage_acc, pieces):
        block_rows, block_codes = pieces
        logits = scores(block_rows)
        row_top = lax.optimization_barrier(jnp.max(logits, axis=1, keepdims=True))
        log_total = row_top + jnp.log(lax.optimization_barrier(jnp.sum(jnp.exp(logits - row_top), axis=1, keepdims=True)))
        probs = jnp.exp(logits - log_total)
        mean_logit = lax.optimization_barrier(jnp.sum(probs * logits, axis=1))
        picked = jnp.take_along_axis(logits, block_codes[:, None].astype(jnp.int32), axis=1)[:, 0]
        return (usage_acc + lax.optimization_barrier(jnp.sum(probs, axis=0)), (log_total[:, 0], mean_logit, log_total[:, 0] - mean_logit, log_total[:, 0] - picked))
    usage_acc, stats = lax.scan(first_pass, jnp.zeros((code_total,), jnp.float32), (block_lat, block_hard))
    log_totals, mean_logits, entropies, crosses = stats
    mean_usage = usage_acc / tokens_total
    log_usage = jnp.log(mean_usage + usage_eps)
    weight_term = log_usage + mean_usage / (mean_usage + usage_eps)
    usage_entropy = -jnp.sum(mean_usage * log_usage)

    def second_pass(code_grad, pieces):
        block_rows, block_codes, cotangent, log_total, mean_logit = pieces
        logits = scores(block_rows)
        probs = jnp.exp(logits - log_total[:, None])
        spread = lax.optimization_barrier(jnp.sum(probs * weight_term[None, :], axis=1))
        columns = lax.broadcasted_iota(jnp.int32, (1, code_total), 1)
        matches = (columns == block_codes[:, None].astype(jnp.int32)).astype(jnp.float32)
        grad_logits = (probs - matches - ENTROPY_WEIGHT * probs * (logits - mean_logit[:, None]) + ENTROPY_WEIGHT * probs * (weight_term[None, :] - spread[:, None])).astype(jnp.bfloat16)
        code_vec = jnp.take(codebook, block_codes.astype(jnp.int32), axis=0).astype(jnp.float32)
        rotated = rotate(block_rows.astype(jnp.float32), code_vec, cotangent.astype(jnp.float32))
        grad_rows = rotated + LOGIT_SCALE * jnp.dot(grad_logits, codebook, preferred_element_type=jnp.float32)
        code_grad = code_grad + LOGIT_SCALE * lax.dot_general(grad_logits, block_rows, (((0,), (0,)), ((), ())), preferred_element_type=jnp.float32)
        return (code_grad, grad_rows)
    code_grad, grad_blocks = lax.scan(second_pass, jnp.zeros((code_total, width), jnp.float32), (block_lat, block_hard, block_up, log_totals, mean_logits))
    token_grad = grad_blocks.reshape(tokens_total, width)
    loss_terms = jnp.stack([jnp.mean(crosses), jnp.mean(entropies), usage_entropy])
    return (token_grad, code_grad, loss_terms)
```

```python
import jax
import jax.numpy as jnp
from jax import lax
from jax.sharding import PartitionSpec as P

LOGIT_SCALE = 5.0
ENTROPY_WEIGHT = 0.5
usage_eps = 1e-06
norm_eps = 1e-06
cos_floor = 0.25
BOTH = ("dp", "code")


def rotate(latent, code_vec, cotangent):
    latent_norm = jnp.sqrt(jnp.sum(latent * latent, axis=1, keepdims=True) + norm_eps)
    code_norm = jnp.sqrt(jnp.sum(code_vec * code_vec, axis=1, keepdims=True) + norm_eps)
    latent_dir = latent / latent_norm
    code_dir = code_vec / code_norm
    cosine = jnp.sum(latent_dir * code_dir, axis=1, keepdims=True)
    summed = latent_dir + code_dir
    along = jnp.sum(summed * cotangent, axis=1, keepdims=True)
    facing = jnp.sum(code_dir * cotangent, axis=1, keepdims=True)
    turned = (
        cotangent
        - summed * along / jnp.maximum(1.0 + cosine, cos_floor)
        + 2.0 * latent_dir * facing
    )
    return code_norm / latent_norm * turned


def local(latents, codebook, hard_code, upstream):
    n_dp = lax.axis_size("dp")
    n_code = lax.axis_size("code")
    dp_i = lax.axis_index("dp")
    code_i = lax.axis_index("code")
    row_count = latents.shape[0]
    code_count = codebook.shape[0]
    tokens_total = row_count * n_dp
    slab = code_count // n_dp
    owned = row_count // n_code
    all_lat = lax.all_gather(latents, "dp", tiled=True)
    all_hard = lax.all_gather(hard_code, "dp", tiled=True)
    my_codes = lax.dynamic_slice_in_dim(codebook, dp_i * slab, slab, axis=0)
    offset = code_i * code_count + dp_i * slab
    logits = LOGIT_SCALE * lax.dot_general(
        all_lat, my_codes, (((1,), (1,)), ((), ())), preferred_element_type=jnp.float32
    )
    columns = lax.broadcasted_iota(jnp.int32, (1, slab), 1)
    target = (all_hard - offset)[:, None]
    matches = columns == target
    picked_local = jnp.sum(jnp.where(matches, logits, 0.0), axis=1)
    row_top = lax.pmax(jnp.max(logits, axis=1), BOTH)
    shifted = jnp.exp(logits - row_top[:, None])
    row_total, moment, picked = lax.psum(
        (jnp.sum(shifted, axis=1), jnp.sum(shifted * logits, axis=1), picked_local), BOTH
    )
    log_total = row_top + jnp.log(row_total)
    mean_logit = moment / row_total
    entropy = log_total - mean_logit
    cross = log_total - picked
    probs = jnp.exp(logits - log_total[:, None])
    mean_usage = jnp.sum(probs, axis=0) / tokens_total
    log_usage = jnp.log(mean_usage + usage_eps)
    weight_term = log_usage + mean_usage / (mean_usage + usage_eps)
    spread, usage_entropy = lax.psum(
        (jnp.sum(probs * weight_term[None, :], axis=1), -jnp.sum(mean_usage * log_usage)), BOTH
    )
    grad_logits = (
        probs
        - matches.astype(jnp.float32)
        - ENTROPY_WEIGHT * probs * (logits - mean_logit[:, None])
        + ENTROPY_WEIGHT * probs * (weight_term[None, :] - spread[:, None])
    ).astype(jnp.bfloat16)
    token_part = LOGIT_SCALE * jnp.dot(grad_logits, my_codes, preferred_element_type=jnp.float32)
    token_sum = lax.psum_scatter(token_part, BOTH, scatter_dimension=0, tiled=True)
    codebook_grad = LOGIT_SCALE * lax.dot_general(
        grad_logits, all_lat, (((0,), (0,)), ((), ())), preferred_element_type=jnp.float32
    )
    shard_target = hard_code - code_i * code_count
    holder = ((shard_target >= 0) & (shard_target < code_count))[:, None]
    picked_vec = jnp.where(
        holder, jnp.take(codebook, jnp.clip(shard_target, 0, code_count - 1), axis=0), 0
    ).astype(jnp.bfloat16)
    code_vec = lax.psum_scatter(picked_vec, "code", scatter_dimension=0, tiled=True)
    own_lat = lax.dynamic_slice_in_dim(latents, code_i * owned, owned, axis=0)
    own_up = lax.dynamic_slice_in_dim(upstream, code_i * owned, owned, axis=0)
    rotated = rotate(
        own_lat.astype(jnp.float32), code_vec.astype(jnp.float32), own_up.astype(jnp.float32)
    )
    token_grad = token_sum + rotated
    loss_terms = jnp.stack(
        [jnp.sum(cross) / tokens_total, jnp.sum(entropy) / tokens_total, usage_entropy]
    )
    return (token_grad, codebook_grad, loss_terms)


def solution(mesh):
    placed = (P("dp", None), P("code", None), P("dp"), P("dp", None))
    return jax.shard_map(
        local,
        mesh=mesh,
        in_specs=placed,
        out_specs=(P(("dp", "code"), None), P(("code", "dp"), None), P()),
        check_vma=False,
    )
```

```python
import jax
import jax.numpy as jnp
from jax import lax
from jax.sharding import PartitionSpec as P

LOGIT_SCALE = 5.0
ENTROPY_WEIGHT = 0.5
usage_eps = 1e-06
norm_eps = 1e-06
cos_floor = 0.25
BOTH = ("dp", "code")


def butterfly(values, axis, count, combine):
    step = 1
    while step < count:
        pairs = [(i, i ^ step) for i in range(count)]
        values = combine(values, lax.ppermute(values, axis, pairs))
        step *= 2
    return values


def butterfly_gather(block, axis, count):
    index = lax.axis_index(axis)
    step = 1
    while step < count:
        pairs = [(i, i ^ step) for i in range(count)]
        other = lax.ppermute(block, axis, pairs)
        low = (index // step) % 2 == 0
        block = jnp.where(low, jnp.concatenate([block, other]), jnp.concatenate([other, block]))
        step *= 2
    return block


def softmax_merge(a, b):
    top = jnp.maximum(a[0], b[0])
    wa = jnp.exp(a[0] - top)
    wb = jnp.exp(b[0] - top)
    return jnp.stack([top, a[1] * wa + b[1] * wb, a[2] * wa + b[2] * wb, a[3] + b[3]])


def is_pow2(n):
    return n & (n - 1) == 0


def rotate(latent, code_vec, cotangent):
    latent_norm = jnp.sqrt(jnp.sum(latent * latent, axis=1, keepdims=True) + norm_eps)
    code_norm = jnp.sqrt(jnp.sum(code_vec * code_vec, axis=1, keepdims=True) + norm_eps)
    latent_dir = latent / latent_norm
    code_dir = code_vec / code_norm
    cosine = jnp.sum(latent_dir * code_dir, axis=1, keepdims=True)
    summed = latent_dir + code_dir
    along = jnp.sum(summed * cotangent, axis=1, keepdims=True)
    facing = jnp.sum(code_dir * cotangent, axis=1, keepdims=True)
    turned = (
        cotangent
        - summed * along / jnp.maximum(1.0 + cosine, cos_floor)
        + 2.0 * latent_dir * facing
    )
    return code_norm / latent_norm * turned


def local(latents, codebook, hard_code, upstream):
    n_dp = lax.axis_size("dp")
    n_code = lax.axis_size("code")
    dp_i = lax.axis_index("dp")
    code_i = lax.axis_index("code")
    row_count = latents.shape[0]
    code_count = codebook.shape[0]
    tokens_total = row_count * n_dp
    slab = code_count // n_dp
    owned = row_count // n_code
    all_lat = lax.all_gather(latents, "dp", tiled=True)
    n_all = n_dp * n_code
    if is_pow2(n_dp):
        all_hard = butterfly_gather(hard_code, "dp", n_dp)
    else:
        all_hard = lax.all_gather(hard_code, "dp", tiled=True)
    my_codes = lax.dynamic_slice_in_dim(codebook, dp_i * slab, slab, axis=0)
    offset = code_i * code_count + dp_i * slab
    logits = LOGIT_SCALE * lax.dot_general(
        all_lat, my_codes, (((1,), (1,)), ((), ())), preferred_element_type=jnp.float32
    )
    columns = lax.broadcasted_iota(jnp.int32, (1, slab), 1)
    target = (all_hard - offset)[:, None]
    matches = columns == target
    picked_local = jnp.sum(jnp.where(matches, logits, 0.0), axis=1)
    local_top = jnp.max(logits, axis=1)
    shifted = jnp.exp(logits - local_top[:, None])
    stats = (local_top, jnp.sum(shifted, axis=1), jnp.sum(shifted * logits, axis=1), picked_local)
    if is_pow2(n_all):
        row_top, row_total, moment, picked = butterfly(jnp.stack(stats), BOTH, n_all, softmax_merge)
    else:
        row_top = lax.pmax(local_top, BOTH)
        scale = jnp.exp(local_top - row_top)
        row_total, moment, picked = lax.psum((stats[1] * scale, stats[2] * scale, stats[3]), BOTH)
    log_total = row_top + jnp.log(row_total)
    mean_logit = moment / row_total
    entropy = log_total - mean_logit
    cross = log_total - picked
    probs = jnp.exp(logits - log_total[:, None])
    mean_usage = jnp.sum(probs, axis=0) / tokens_total
    log_usage = jnp.log(mean_usage + usage_eps)
    weight_term = log_usage + mean_usage / (mean_usage + usage_eps)
    spread_parts = (jnp.sum(probs * weight_term[None, :], axis=1), -jnp.sum(mean_usage * log_usage))
    if is_pow2(n_all):
        joined = jnp.concatenate([spread_parts[0], spread_parts[1][None]])
        joined = butterfly(joined, BOTH, n_all, jnp.add)
        spread, usage_entropy = joined[:-1], joined[-1]
    else:
        spread, usage_entropy = lax.psum(spread_parts, BOTH)
    grad_logits = (
        probs
        - matches.astype(jnp.float32)
        - ENTROPY_WEIGHT * probs * (logits - mean_logit[:, None])
        + ENTROPY_WEIGHT * probs * (weight_term[None, :] - spread[:, None])
    ).astype(jnp.bfloat16)
    token_part = LOGIT_SCALE * jnp.dot(grad_logits, my_codes, preferred_element_type=jnp.float32)
    token_sum = lax.psum_scatter(token_part, BOTH, scatter_dimension=0, tiled=True)
    codebook_grad = LOGIT_SCALE * lax.dot_general(
        grad_logits, all_lat, (((0,), (0,)), ((), ())), preferred_element_type=jnp.float32
    )
    shard_target = hard_code - code_i * code_count
    holder = ((shard_target >= 0) & (shard_target < code_count))[:, None]
    picked_vec = jnp.where(
        holder, jnp.take(codebook, jnp.clip(shard_target, 0, code_count - 1), axis=0), 0
    ).astype(jnp.bfloat16)
    code_vec = lax.psum_scatter(picked_vec, "code", scatter_dimension=0, tiled=True)
    own_lat = lax.dynamic_slice_in_dim(latents, code_i * owned, owned, axis=0)
    own_up = lax.dynamic_slice_in_dim(upstream, code_i * owned, owned, axis=0)
    rotated = rotate(
        own_lat.astype(jnp.float32), code_vec.astype(jnp.float32), own_up.astype(jnp.float32)
    )
    token_grad = token_sum + rotated
    loss_terms = jnp.stack(
        [jnp.sum(cross) / tokens_total, jnp.sum(entropy) / tokens_total, usage_entropy]
    )
    return (token_grad, codebook_grad, loss_terms)


def solution(mesh):
    placed = (P("dp", None), P("code", None), P("dp"), P("dp", None))
    return jax.shard_map(
        local,
        mesh=mesh,
        in_specs=placed,
        out_specs=(P(("dp", "code"), None), P(("code", "dp"), None), P()),
        check_vma=False,
    )
```

```python
import jax
import jax.numpy as jnp
from jax import lax
from jax.experimental import pallas as pl
from jax.experimental.pallas import tpu as pltpu
from jax.sharding import PartitionSpec as P
import functools

LOGIT_SCALE = 5.0
ENTROPY_WEIGHT = 0.5
usage_eps = 1e-06
norm_eps = 1e-06
cos_floor = 0.25
BOTH = ("dp", "code")
TM = 512
TN = 1024
VMEM = 48 * 1024 * 1024


def _logits(lat_ref, cb_ref):
    return LOGIT_SCALE * lax.dot_general(
        lat_ref[...], cb_ref[...], (((1,), (1,)), ((), ())), preferred_element_type=jnp.float32
    )


def _stats_kernel(lat_ref, cb_ref, tgt_ref, m_ref, s_ref, t_ref, p_ref, tn):
    j = pl.program_id(1)

    @pl.when(j == 0)
    def _():
        m_ref[...] = jnp.full(m_ref.shape, -jnp.inf, jnp.float32)
        s_ref[...] = jnp.zeros(s_ref.shape, jnp.float32)
        t_ref[...] = jnp.zeros(t_ref.shape, jnp.float32)
        p_ref[...] = jnp.zeros(p_ref.shape, jnp.float32)

    logits = _logits(lat_ref, cb_ref)
    m_old = m_ref[...]
    m_new = jnp.maximum(m_old, jnp.max(logits, axis=1, keepdims=True))
    rescale = jnp.exp(m_old - m_new)
    shifted = jnp.exp(logits - m_new)
    cols = j * tn + lax.broadcasted_iota(jnp.int32, logits.shape, 1)
    hit = cols == tgt_ref[...]
    m_ref[...] = m_new
    s_ref[...] = s_ref[...] * rescale + jnp.sum(shifted, axis=1, keepdims=True)
    t_ref[...] = t_ref[...] * rescale + jnp.sum(shifted * logits, axis=1, keepdims=True)
    p_ref[...] = p_ref[...] + jnp.sum(jnp.where(hit, logits, 0.0), axis=1, keepdims=True)


def row_stats(lat, cb, tgt, interpret=False):
    t_all, d = lat.shape
    s_all = cb.shape[0]
    tm, tn = min(TM, t_all), min(TN, s_all)
    row = pl.BlockSpec((tm, 1), lambda i, j: (i, 0))
    col_out = jax.ShapeDtypeStruct((t_all, 1), jnp.float32)
    return pl.pallas_call(
        functools.partial(_stats_kernel, tn=tn),
        grid=(t_all // tm, s_all // tn),
        in_specs=[
            pl.BlockSpec((tm, d), lambda i, j: (i, 0)),
            pl.BlockSpec((tn, d), lambda i, j: (j, 0)),
            row,
        ],
        out_specs=[row, row, row, row],
        out_shape=[col_out] * 4,
        compiler_params=pltpu.CompilerParams(
            dimension_semantics=("arbitrary", "arbitrary"), vmem_limit_bytes=VMEM
        ),
        interpret=interpret,
    )(lat, cb, tgt)


def _usage_kernel(lat_ref, cb_ref, lt_ref, out_ref):
    i = pl.program_id(1)
    probs = jnp.exp(_logits(lat_ref, cb_ref) - lt_ref[...])
    col = jnp.sum(probs, axis=0, keepdims=True)

    @pl.when(i == 0)
    def _():
        out_ref[...] = col

    @pl.when(i > 0)
    def _():
        out_ref[...] = out_ref[...] + col


def usage_sums(lat, cb, lt, interpret=False):
    t_all, d = lat.shape
    s_all = cb.shape[0]
    tm, tn = min(TM, t_all), min(TN, s_all)
    return pl.pallas_call(
        _usage_kernel,
        grid=(s_all // tn, t_all // tm),
        in_specs=[
            pl.BlockSpec((tm, d), lambda j, i: (i, 0)),
            pl.BlockSpec((tn, d), lambda j, i: (j, 0)),
            pl.BlockSpec((tm, 1), lambda j, i: (i, 0)),
        ],
        out_specs=pl.BlockSpec((1, tn), lambda j, i: (0, j)),
        out_shape=jax.ShapeDtypeStruct((1, s_all), jnp.float32),
        compiler_params=pltpu.CompilerParams(
            dimension_semantics=("arbitrary", "arbitrary"), vmem_limit_bytes=VMEM
        ),
        interpret=interpret,
    )(lat, cb, lt)


def _spread_kernel(lat_ref, cb_ref, lt_ref, w_ref, out_ref):
    j = pl.program_id(1)
    probs = jnp.exp(_logits(lat_ref, cb_ref) - lt_ref[...])
    part = jnp.sum(probs * w_ref[...], axis=1, keepdims=True)

    @pl.when(j == 0)
    def _():
        out_ref[...] = part

    @pl.when(j > 0)
    def _():
        out_ref[...] = out_ref[...] + part


def spread_sums(lat, cb, lt, w, interpret=False):
    t_all, d = lat.shape
    s_all = cb.shape[0]
    tm, tn = min(TM, t_all), min(TN, s_all)
    return pl.pallas_call(
        _spread_kernel,
        grid=(t_all // tm, s_all // tn),
        in_specs=[
            pl.BlockSpec((tm, d), lambda i, j: (i, 0)),
            pl.BlockSpec((tn, d), lambda i, j: (j, 0)),
            pl.BlockSpec((tm, 1), lambda i, j: (i, 0)),
            pl.BlockSpec((1, tn), lambda i, j: (0, j)),
        ],
        out_specs=pl.BlockSpec((tm, 1), lambda i, j: (i, 0)),
        out_shape=jax.ShapeDtypeStruct((t_all, 1), jnp.float32),
        compiler_params=pltpu.CompilerParams(
            dimension_semantics=("arbitrary", "arbitrary"), vmem_limit_bytes=VMEM
        ),
        interpret=interpret,
    )(lat, cb, lt, w)


def _grad_kernel(lat_ref, cb_ref, lt_ref, rowc_ref, tgt_ref, hw_ref, tok_ref, cbg_ref, tm, tn):
    j = pl.program_id(0)
    i = pl.program_id(1)
    logits = _logits(lat_ref, cb_ref)
    probs = jnp.exp(logits - lt_ref[...])
    cols = j * tn + lax.broadcasted_iota(jnp.int32, logits.shape, 1)
    hit = (cols == tgt_ref[...]).astype(jnp.float32)
    grad = (probs * (rowc_ref[...] + hw_ref[...] - 0.5 * logits) - hit).astype(jnp.bfloat16)
    tok = jnp.dot(grad, cb_ref[...], preferred_element_type=jnp.float32)
    cbg = lax.dot_general(
        grad, lat_ref[...], (((0,), (0,)), ((), ())), preferred_element_type=jnp.float32
    )
    rows = pl.ds(pl.multiple_of(i * tm, tm), tm)

    @pl.when(j == 0)
    def _():
        tok_ref[rows, :] = tok

    @pl.when(j > 0)
    def _():
        tok_ref[rows, :] = tok_ref[rows, :] + tok

    @pl.when(i == 0)
    def _():
        cbg_ref[...] = cbg

    @pl.when(i > 0)
    def _():
        cbg_ref[...] = cbg_ref[...] + cbg


def grads(lat, cb, lt, rowc, tgt, hw, interpret=False):
    t_all, d = lat.shape
    s_all = cb.shape[0]
    tm, tn = min(TM, t_all), min(TN, s_all)
    row = pl.BlockSpec((tm, 1), lambda j, i: (i, 0))
    return pl.pallas_call(
        functools.partial(_grad_kernel, tm=tm, tn=tn),
        grid=(s_all // tn, t_all // tm),
        in_specs=[
            pl.BlockSpec((tm, d), lambda j, i: (i, 0)),
            pl.BlockSpec((tn, d), lambda j, i: (j, 0)),
            row,
            row,
            row,
            pl.BlockSpec((1, tn), lambda j, i: (0, j)),
        ],
        out_specs=[
            pl.BlockSpec((t_all, d), lambda j, i: (0, 0)),
            pl.BlockSpec((tn, d), lambda j, i: (j, 0)),
        ],
        out_shape=[
            jax.ShapeDtypeStruct((t_all, d), jnp.float32),
            jax.ShapeDtypeStruct((s_all, d), jnp.float32),
        ],
        compiler_params=pltpu.CompilerParams(
            dimension_semantics=("arbitrary", "arbitrary"), vmem_limit_bytes=VMEM
        ),
        interpret=interpret,
    )(lat, cb, lt, rowc, tgt, hw)


def butterfly(values, axis, count, combine):
    step = 1
    while step < count:
        pairs = [(i, i ^ step) for i in range(count)]
        values = combine(values, lax.ppermute(values, axis, pairs))
        step *= 2
    return values


def butterfly_gather(block, axis, count):
    index = lax.axis_index(axis)
    step = 1
    while step < count:
        pairs = [(i, i ^ step) for i in range(count)]
        other = lax.ppermute(block, axis, pairs)
        low = (index // step) % 2 == 0
        block = jnp.where(low, jnp.concatenate([block, other]), jnp.concatenate([other, block]))
        step *= 2
    return block


def softmax_merge(a, b):
    top = jnp.maximum(a[0], b[0])
    wa = jnp.exp(a[0] - top)
    wb = jnp.exp(b[0] - top)
    return jnp.stack([top, a[1] * wa + b[1] * wb, a[2] * wa + b[2] * wb, a[3] + b[3]])


def is_pow2(n):
    return n & (n - 1) == 0


def rotate(latent, code_vec, cotangent):
    latent_norm = jnp.sqrt(jnp.sum(latent * latent, axis=1, keepdims=True) + norm_eps)
    code_norm = jnp.sqrt(jnp.sum(code_vec * code_vec, axis=1, keepdims=True) + norm_eps)
    latent_dir = latent / latent_norm
    code_dir = code_vec / code_norm
    cosine = jnp.sum(latent_dir * code_dir, axis=1, keepdims=True)
    summed = latent_dir + code_dir
    along = jnp.sum(summed * cotangent, axis=1, keepdims=True)
    facing = jnp.sum(code_dir * cotangent, axis=1, keepdims=True)
    turned = (
        cotangent
        - summed * along / jnp.maximum(1.0 + cosine, cos_floor)
        + 2.0 * latent_dir * facing
    )
    return code_norm / latent_norm * turned


def local(latents, codebook, hard_code, upstream):
    n_dp = lax.axis_size("dp")
    n_code = lax.axis_size("code")
    dp_i = lax.axis_index("dp")
    code_i = lax.axis_index("code")
    row_count = latents.shape[0]
    code_count = codebook.shape[0]
    tokens_total = row_count * n_dp
    slab = code_count // n_dp
    owned = row_count // n_code
    all_lat = lax.all_gather(latents, "dp", tiled=True)
    n_all = n_dp * n_code
    if is_pow2(n_dp):
        all_hard = butterfly_gather(hard_code, "dp", n_dp)
    else:
        all_hard = lax.all_gather(hard_code, "dp", tiled=True)
    my_codes = lax.dynamic_slice_in_dim(codebook, dp_i * slab, slab, axis=0)
    offset = code_i * code_count + dp_i * slab
    target = (all_hard - offset)[:, None].astype(jnp.int32)
    stats = jnp.stack([v[:, 0] for v in row_stats(all_lat, my_codes, target)])
    if is_pow2(n_all):
        row_top, row_total, moment, picked = butterfly(stats, BOTH, n_all, softmax_merge)
    else:
        row_top = lax.pmax(stats[0], BOTH)
        scale = jnp.exp(stats[0] - row_top)
        row_total, moment, picked = lax.psum((stats[1] * scale, stats[2] * scale, stats[3]), BOTH)
    log_total = row_top + jnp.log(row_total)
    mean_logit = moment / row_total
    entropy = log_total - mean_logit
    cross = log_total - picked
    mean_usage = usage_sums(all_lat, my_codes, log_total[:, None])[0] / tokens_total
    log_usage = jnp.log(mean_usage + usage_eps)
    weight_term = log_usage + mean_usage / (mean_usage + usage_eps)
    spread_parts = (
        spread_sums(all_lat, my_codes, log_total[:, None], weight_term[None, :])[:, 0],
        -jnp.sum(mean_usage * log_usage),
    )
    if is_pow2(n_all):
        joined = jnp.concatenate([spread_parts[0], spread_parts[1][None]])
        joined = butterfly(joined, BOTH, n_all, jnp.add)
        spread, usage_entropy = joined[:-1], joined[-1]
    else:
        spread, usage_entropy = lax.psum(spread_parts, BOTH)
    row_coef = 1.0 + ENTROPY_WEIGHT * (mean_logit - spread)
    token_acc, code_acc = grads(
        all_lat, my_codes, log_total[:, None], row_coef[:, None], target,
        ENTROPY_WEIGHT * weight_term[None, :],
    )
    token_sum = lax.psum_scatter(LOGIT_SCALE * token_acc, BOTH, scatter_dimension=0, tiled=True)
    codebook_grad = LOGIT_SCALE * code_acc
    shard_target = hard_code - code_i * code_count
    holder = ((shard_target >= 0) & (shard_target < code_count))[:, None]
    picked_vec = jnp.where(
        holder, jnp.take(codebook, jnp.clip(shard_target, 0, code_count - 1), axis=0), 0
    ).astype(jnp.bfloat16)
    code_vec = lax.psum_scatter(picked_vec, "code", scatter_dimension=0, tiled=True)
    own_lat = lax.dynamic_slice_in_dim(latents, code_i * owned, owned, axis=0)
    own_up = lax.dynamic_slice_in_dim(upstream, code_i * owned, owned, axis=0)
    rotated = rotate(
        own_lat.astype(jnp.float32), code_vec.astype(jnp.float32), own_up.astype(jnp.float32)
    )
    token_grad = token_sum + rotated
    loss_terms = jnp.stack(
        [jnp.sum(cross) / tokens_total, jnp.sum(entropy) / tokens_total, usage_entropy]
    )
    return (token_grad, codebook_grad, loss_terms)


def solution(mesh):
    placed = (P("dp", None), P("code", None), P("dp"), P("dp", None))
    return jax.shard_map(
        local,
        mesh=mesh,
        in_specs=placed,
        out_specs=(P(("dp", "code"), None), P(("code", "dp"), None), P()),
        check_vma=False,
    )
```

```python
import jax
import jax.numpy as jnp
from jax import lax
from jax.experimental import pallas as pl
from jax.experimental.pallas import tpu as pltpu
from jax.sharding import PartitionSpec as P
import functools

LOGIT_SCALE = 5.0
ENTROPY_WEIGHT = 0.5
usage_eps = 1e-06
norm_eps = 1e-06
cos_floor = 0.25
BOTH = ("dp", "code")
TM = 512
TN = 1024
VMEM = 48 * 1024 * 1024


def _logits(lat_ref, cb_ref):
    return LOGIT_SCALE * lax.dot_general(
        lat_ref[...], cb_ref[...], (((1,), (1,)), ((), ())), preferred_element_type=jnp.float32
    )


def _lane_groups(x):
    return [x[:, g * 128:(g + 1) * 128] for g in range(x.shape[1] // 128)]


def _stats_kernel(lat_ref, cb_ref, m_ref, s_ref, t_ref):
    j = pl.program_id(1)

    @pl.when(j == 0)
    def _():
        m_ref[...] = jnp.full(m_ref.shape, -jnp.inf, jnp.float32)
        s_ref[...] = jnp.zeros(s_ref.shape, jnp.float32)
        t_ref[...] = jnp.zeros(t_ref.shape, jnp.float32)

    groups = _lane_groups(_logits(lat_ref, cb_ref))
    m_old = m_ref[...]
    m_new = functools.reduce(jnp.maximum, groups, m_old)
    rescale = jnp.exp(m_old - m_new)
    s_acc = s_ref[...] * rescale
    t_acc = t_ref[...] * rescale
    for g in groups:
        e = jnp.exp(g - m_new)
        s_acc = s_acc + e
        t_acc = t_acc + e * g
    m_ref[...] = m_new
    s_ref[...] = s_acc
    t_ref[...] = t_acc


def row_stats(lat, cb, interpret=False):
    t_all, d = lat.shape
    s_all = cb.shape[0]
    tm, tn = min(TM, t_all), min(TN, s_all)
    row = pl.BlockSpec((tm, 128), lambda i, j: (i, 0))
    lanes = jax.ShapeDtypeStruct((t_all, 128), jnp.float32)
    return pl.pallas_call(
        _stats_kernel,
        grid=(t_all // tm, s_all // tn),
        in_specs=[
            pl.BlockSpec((tm, d), lambda i, j: (i, 0)),
            pl.BlockSpec((tn, d), lambda i, j: (j, 0)),
        ],
        out_specs=[row, row, row],
        out_shape=[lanes] * 3,
        compiler_params=pltpu.CompilerParams(
            dimension_semantics=("arbitrary", "arbitrary"), vmem_limit_bytes=VMEM
        ),
        interpret=interpret,
    )(lat, cb)


def _usage_kernel(lat_ref, cb_ref, lt_ref, out_ref):
    i = pl.program_id(1)
    probs = jnp.exp(_logits(lat_ref, cb_ref) - lt_ref[...])
    col = jnp.sum(probs, axis=0, keepdims=True)

    @pl.when(i == 0)
    def _():
        out_ref[...] = col

    @pl.when(i > 0)
    def _():
        out_ref[...] = out_ref[...] + col


def usage_sums(lat, cb, lt, interpret=False):
    t_all, d = lat.shape
    s_all = cb.shape[0]
    tm, tn = min(TM, t_all), min(TN, s_all)
    return pl.pallas_call(
        _usage_kernel,
        grid=(s_all // tn, t_all // tm),
        in_specs=[
            pl.BlockSpec((tm, d), lambda j, i: (i, 0)),
            pl.BlockSpec((tn, d), lambda j, i: (j, 0)),
            pl.BlockSpec((tm, 1), lambda j, i: (i, 0)),
        ],
        out_specs=pl.BlockSpec((1, tn), lambda j, i: (0, j)),
        out_shape=jax.ShapeDtypeStruct((1, s_all), jnp.float32),
        compiler_params=pltpu.CompilerParams(
            dimension_semantics=("arbitrary", "arbitrary"), vmem_limit_bytes=VMEM
        ),
        interpret=interpret,
    )(lat, cb, lt)


def _spread_kernel(lat_ref, cb_ref, lt_ref, w_ref, out_ref):
    j = pl.program_id(1)
    groups = _lane_groups(jnp.exp(_logits(lat_ref, cb_ref) - lt_ref[...]))
    weights = _lane_groups(w_ref[...])
    part = groups[0] * weights[0]
    for g, w in zip(groups[1:], weights[1:]):
        part = part + g * w

    @pl.when(j == 0)
    def _():
        out_ref[...] = part

    @pl.when(j > 0)
    def _():
        out_ref[...] = out_ref[...] + part


def spread_sums(lat, cb, lt, w, interpret=False):
    t_all, d = lat.shape
    s_all = cb.shape[0]
    tm, tn = min(TM, t_all), min(TN, s_all)
    return pl.pallas_call(
        _spread_kernel,
        grid=(t_all // tm, s_all // tn),
        in_specs=[
            pl.BlockSpec((tm, d), lambda i, j: (i, 0)),
            pl.BlockSpec((tn, d), lambda i, j: (j, 0)),
            pl.BlockSpec((tm, 1), lambda i, j: (i, 0)),
            pl.BlockSpec((1, tn), lambda i, j: (0, j)),
        ],
        out_specs=pl.BlockSpec((tm, 128), lambda i, j: (i, 0)),
        out_shape=jax.ShapeDtypeStruct((t_all, 128), jnp.float32),
        compiler_params=pltpu.CompilerParams(
            dimension_semantics=("arbitrary", "arbitrary"), vmem_limit_bytes=VMEM
        ),
        interpret=interpret,
    )(lat, cb, lt, w)


def _grad_kernel(lat_ref, cb_ref, lt_ref, rowc_ref, tgt_ref, hw_ref, *refs, tm, tn, carry):
    if carry:
        prev_ref, tok_ref, cbg_ref = refs
    else:
        tok_ref, cbg_ref = refs
    j = pl.program_id(0)
    i = pl.program_id(1)
    logits = _logits(lat_ref, cb_ref)
    probs = jnp.exp(logits - lt_ref[...])
    cols = j * tn + lax.broadcasted_iota(jnp.int32, logits.shape, 1)
    hit = (cols == tgt_ref[...]).astype(jnp.float32)
    grad = (probs * (rowc_ref[...] + hw_ref[...] - 0.5 * logits) - hit).astype(jnp.bfloat16)
    tok = jnp.dot(grad, cb_ref[...], preferred_element_type=jnp.float32)
    cbg = lax.dot_general(
        grad, lat_ref[...], (((0,), (0,)), ((), ())), preferred_element_type=jnp.float32
    )
    rows = pl.ds(pl.multiple_of(i * tm, tm), tm)

    @pl.when(j == 0)
    def _():
        tok_ref[rows, :] = tok

    @pl.when(j > 0)
    def _():
        tok_ref[rows, :] = tok_ref[rows, :] + tok

    @pl.when(i == 0)
    def _():
        cbg_ref[...] = prev_ref[...] + cbg if carry else cbg

    @pl.when(i > 0)
    def _():
        cbg_ref[...] = cbg_ref[...] + cbg


def grads(lat, cb, lt, rowc, tgt, hw, prev=None, interpret=False):
    t_all, d = lat.shape
    s_all = cb.shape[0]
    tm, tn = min(TM, t_all), min(TN, s_all)
    row = pl.BlockSpec((tm, 1), lambda j, i: (i, 0))
    return pl.pallas_call(
        functools.partial(_grad_kernel, tm=tm, tn=tn, carry=prev is not None),
        grid=(s_all // tn, t_all // tm),
        in_specs=[
            pl.BlockSpec((tm, d), lambda j, i: (i, 0)),
            pl.BlockSpec((tn, d), lambda j, i: (j, 0)),
            row,
            row,
            row,
            pl.BlockSpec((1, tn), lambda j, i: (0, j)),
        ] + ([] if prev is None else [pl.BlockSpec((tn, d), lambda j, i: (j, 0))]),
        out_specs=[
            pl.BlockSpec((t_all, d), lambda j, i: (0, 0)),
            pl.BlockSpec((tn, d), lambda j, i: (j, 0)),
        ],
        out_shape=[
            jax.ShapeDtypeStruct((t_all, d), jnp.float32),
            jax.ShapeDtypeStruct((s_all, d), jnp.float32),
        ],
        compiler_params=pltpu.CompilerParams(
            dimension_semantics=("arbitrary", "arbitrary"), vmem_limit_bytes=VMEM
        ),
        input_output_aliases={} if prev is None else {6: 1},
        interpret=interpret,
    )(lat, cb, lt, rowc, tgt, hw, *([] if prev is None else [prev]))


def butterfly(values, axis, count, combine):
    step = 1
    while step < count:
        pairs = [(i, i ^ step) for i in range(count)]
        values = combine(values, lax.ppermute(values, axis, pairs))
        step *= 2
    return values


def butterfly_gather(block, axis, count):
    index = lax.axis_index(axis)
    step = 1
    while step < count:
        pairs = [(i, i ^ step) for i in range(count)]
        other = lax.ppermute(block, axis, pairs)
        low = (index // step) % 2 == 0
        block = jnp.where(low, jnp.concatenate([block, other]), jnp.concatenate([other, block]))
        step *= 2
    return block


def softmax_merge(a, b):
    top = jnp.maximum(a[0], b[0])
    wa = jnp.exp(a[0] - top)
    wb = jnp.exp(b[0] - top)
    return jnp.stack([top, a[1] * wa + b[1] * wb, a[2] * wa + b[2] * wb])


def is_pow2(n):
    return n & (n - 1) == 0


def rotate(latent, code_vec, cotangent):
    latent_norm = jnp.sqrt(jnp.sum(latent * latent, axis=1, keepdims=True) + norm_eps)
    code_norm = jnp.sqrt(jnp.sum(code_vec * code_vec, axis=1, keepdims=True) + norm_eps)
    latent_dir = latent / latent_norm
    code_dir = code_vec / code_norm
    cosine = jnp.sum(latent_dir * code_dir, axis=1, keepdims=True)
    summed = latent_dir + code_dir
    along = jnp.sum(summed * cotangent, axis=1, keepdims=True)
    facing = jnp.sum(code_dir * cotangent, axis=1, keepdims=True)
    turned = (
        cotangent
        - summed * along / jnp.maximum(1.0 + cosine, cos_floor)
        + 2.0 * latent_dir * facing
    )
    return code_norm / latent_norm * turned


def local(latents, codebook, hard_code, upstream):
    n_dp = lax.axis_size("dp")
    n_code = lax.axis_size("code")
    n_all = n_dp * n_code
    dp_i = lax.axis_index("dp")
    code_i = lax.axis_index("code")
    row_count = latents.shape[0]
    code_count = codebook.shape[0]
    width = latents.shape[1]
    tokens_total = row_count * n_dp
    slab = code_count // n_dp
    owned = row_count // n_code
    all_lat = lax.all_gather(latents, "dp", tiled=True)
    if is_pow2(n_dp):
        all_hard = butterfly_gather(hard_code, "dp", n_dp)
    else:
        all_hard = lax.all_gather(hard_code, "dp", tiled=True)
    my_codes = lax.dynamic_slice_in_dim(codebook, dp_i * slab, slab, axis=0)
    offset = code_i * code_count + dp_i * slab

    shard_target = hard_code - code_i * code_count
    holder = ((shard_target >= 0) & (shard_target < code_count))[:, None]
    picked_vec = jnp.where(
        holder, jnp.take(codebook, jnp.clip(shard_target, 0, code_count - 1), axis=0), 0
    ).astype(jnp.bfloat16)
    code_vec = lax.psum_scatter(picked_vec, "code", scatter_dimension=0, tiled=True).astype(jnp.float32)
    own_lat = lax.dynamic_slice_in_dim(latents, code_i * owned, owned, axis=0).astype(jnp.float32)
    own_up = lax.dynamic_slice_in_dim(upstream, code_i * owned, owned, axis=0).astype(jnp.float32)
    rotated = rotate(own_lat, code_vec, own_up)
    picked_sum = jnp.sum(LOGIT_SCALE * jnp.sum(own_lat * code_vec, axis=1))

    lane_top, lane_total, lane_moment = row_stats(all_lat, my_codes)
    local_top = jnp.max(lane_top, axis=1)
    lane_scale = jnp.exp(lane_top - local_top[:, None])
    stats = jnp.stack([
        local_top, jnp.sum(lane_total * lane_scale, axis=1), jnp.sum(lane_moment * lane_scale, axis=1)
    ])
    if is_pow2(n_all):
        row_top, row_total, moment = butterfly(stats, BOTH, n_all, softmax_merge)
    else:
        row_top = lax.pmax(stats[0], BOTH)
        scale = jnp.exp(stats[0] - row_top)
        row_total, moment = lax.psum((stats[1] * scale, stats[2] * scale), BOTH)
    log_total = row_top + jnp.log(row_total)
    mean_logit = moment / row_total
    entropy = log_total - mean_logit
    mean_usage = usage_sums(all_lat, my_codes, log_total[:, None])[0] / tokens_total
    log_usage = jnp.log(mean_usage + usage_eps)
    weight_term = log_usage + mean_usage / (mean_usage + usage_eps)
    spread_local = jnp.sum(spread_sums(all_lat, my_codes, log_total[:, None], weight_term[None, :]), axis=1)
    extras = jnp.stack([-jnp.sum(mean_usage * log_usage), picked_sum])
    joined = jnp.concatenate([spread_local, extras])
    if is_pow2(n_all):
        joined = butterfly(joined, BOTH, n_all, jnp.add)
    else:
        joined = lax.psum(joined, BOTH)
    spread, usage_entropy, picked_total = joined[:-2], joined[-2], joined[-1]

    row_coef = 1.0 + ENTROPY_WEIGHT * (mean_logit - spread)
    target = (all_hard - offset).astype(jnp.int32)
    chunks = 4 if owned % 4 == 0 and (tokens_total // 4) % min(TM, tokens_total // 4) == 0 else 1
    piece = owned // chunks

    def reorder(x):
        x = x.reshape((n_all, chunks, piece) + x.shape[1:])
        return jnp.swapaxes(x, 0, 1).reshape((chunks, n_all * piece) + x.shape[3:])

    lat_c, lt_c, coef_c, tgt_c = (
        reorder(v) for v in (all_lat, log_total[:, None], row_coef[:, None], target[:, None])
    )
    half_weight = ENTROPY_WEIGHT * weight_term[None, :]
    code_acc = None
    parts = []
    for q in range(chunks):
        token_acc, code_acc = grads(
            lat_c[q], my_codes, lt_c[q], coef_c[q], tgt_c[q], half_weight, prev=code_acc
        )
        parts.append(
            lax.psum_scatter(LOGIT_SCALE * token_acc, BOTH, scatter_dimension=0, tiled=True)
        )
    token_sum = jnp.concatenate(parts, axis=0)
    codebook_grad = LOGIT_SCALE * code_acc
    token_grad = token_sum + rotated
    loss_terms = jnp.stack([
        (jnp.sum(log_total) - picked_total) / tokens_total,
        jnp.sum(entropy) / tokens_total,
        usage_entropy,
    ])
    return (token_grad, codebook_grad, loss_terms)


def solution(mesh):
    placed = (P("dp", None), P("code", None), P("dp"), P("dp", None))
    return jax.shard_map(
        local,
        mesh=mesh,
        in_specs=placed,
        out_specs=(P(("dp", "code"), None), P(("code", "dp"), None), P()),
        check_vma=False,
    )
```

```python
import jax
import jax.numpy as jnp
from jax import lax
from jax.experimental import pallas as pl
from jax.experimental.pallas import tpu as pltpu
from jax.sharding import PartitionSpec as P
import functools

LOGIT_SCALE = 5.0
ENTROPY_WEIGHT = 0.5
usage_eps = 1e-06
norm_eps = 1e-06
cos_floor = 0.25
BOTH = ("dp", "code")
TM = 512
TN = 2048
VMEM = 48 * 1024 * 1024


def _logits(lat_ref, cb_ref):
    return LOGIT_SCALE * lax.dot_general(
        lat_ref[...], cb_ref[...], (((1,), (1,)), ((), ())), preferred_element_type=jnp.float32
    )


def _lane_groups(x):
    return [x[:, g * 128:(g + 1) * 128] for g in range(x.shape[1] // 128)]


def _stats_kernel(lat_ref, cb_ref, m_ref, s_ref, t_ref):
    j = pl.program_id(1)

    @pl.when(j == 0)
    def _():
        m_ref[...] = jnp.full(m_ref.shape, -jnp.inf, jnp.float32)
        s_ref[...] = jnp.zeros(s_ref.shape, jnp.float32)
        t_ref[...] = jnp.zeros(t_ref.shape, jnp.float32)

    groups = _lane_groups(_logits(lat_ref, cb_ref))
    m_old = m_ref[...]
    m_new = functools.reduce(jnp.maximum, groups, m_old)
    rescale = jnp.exp(m_old - m_new)
    s_acc = s_ref[...] * rescale
    t_acc = t_ref[...] * rescale
    for g in groups:
        e = jnp.exp(g - m_new)
        s_acc = s_acc + e
        t_acc = t_acc + e * g
    m_ref[...] = m_new
    s_ref[...] = s_acc
    t_ref[...] = t_acc


def row_stats(lat, cb, interpret=False):
    t_all, d = lat.shape
    s_all = cb.shape[0]
    tm, tn = min(TM, t_all), min(TN, s_all)
    row = pl.BlockSpec((tm, 128), lambda i, j: (i, 0))
    lanes = jax.ShapeDtypeStruct((t_all, 128), jnp.float32)
    return pl.pallas_call(
        _stats_kernel,
        grid=(t_all // tm, s_all // tn),
        in_specs=[
            pl.BlockSpec((tm, d), lambda i, j: (i, 0)),
            pl.BlockSpec((tn, d), lambda i, j: (j, 0)),
        ],
        out_specs=[row, row, row],
        out_shape=[lanes] * 3,
        compiler_params=pltpu.CompilerParams(
            dimension_semantics=("arbitrary", "arbitrary"), vmem_limit_bytes=VMEM
        ),
        interpret=interpret,
    )(lat, cb)


def _usage_kernel(lat_ref, cb_ref, lt_ref, out_ref):
    i = pl.program_id(1)
    probs = jnp.exp(_logits(lat_ref, cb_ref) - lt_ref[...])
    col = jnp.sum(probs, axis=0, keepdims=True)

    @pl.when(i == 0)
    def _():
        out_ref[...] = col

    @pl.when(i > 0)
    def _():
        out_ref[...] = out_ref[...] + col


def usage_sums(lat, cb, lt, interpret=False):
    t_all, d = lat.shape
    s_all = cb.shape[0]
    tm, tn = min(TM, t_all), min(TN, s_all)
    return pl.pallas_call(
        _usage_kernel,
        grid=(s_all // tn, t_all // tm),
        in_specs=[
            pl.BlockSpec((tm, d), lambda j, i: (i, 0)),
            pl.BlockSpec((tn, d), lambda j, i: (j, 0)),
            pl.BlockSpec((tm, 1), lambda j, i: (i, 0)),
        ],
        out_specs=pl.BlockSpec((1, tn), lambda j, i: (0, j)),
        out_shape=jax.ShapeDtypeStruct((1, s_all), jnp.float32),
        compiler_params=pltpu.CompilerParams(
            dimension_semantics=("arbitrary", "arbitrary"), vmem_limit_bytes=VMEM
        ),
        interpret=interpret,
    )(lat, cb, lt)


def _spread_kernel(lat_ref, cb_ref, lt_ref, w_ref, out_ref):
    j = pl.program_id(1)
    groups = _lane_groups(jnp.exp(_logits(lat_ref, cb_ref) - lt_ref[...]))
    weights = _lane_groups(w_ref[...])
    part = groups[0] * weights[0]
    for g, w in zip(groups[1:], weights[1:]):
        part = part + g * w

    @pl.when(j == 0)
    def _():
        out_ref[...] = part

    @pl.when(j > 0)
    def _():
        out_ref[...] = out_ref[...] + part


def spread_sums(lat, cb, lt, w, interpret=False):
    t_all, d = lat.shape
    s_all = cb.shape[0]
    tm, tn = min(TM, t_all), min(TN, s_all)
    return pl.pallas_call(
        _spread_kernel,
        grid=(t_all // tm, s_all // tn),
        in_specs=[
            pl.BlockSpec((tm, d), lambda i, j: (i, 0)),
            pl.BlockSpec((tn, d), lambda i, j: (j, 0)),
            pl.BlockSpec((tm, 1), lambda i, j: (i, 0)),
            pl.BlockSpec((1, tn), lambda i, j: (0, j)),
        ],
        out_specs=pl.BlockSpec((tm, 128), lambda i, j: (i, 0)),
        out_shape=jax.ShapeDtypeStruct((t_all, 128), jnp.float32),
        compiler_params=pltpu.CompilerParams(
            dimension_semantics=("arbitrary", "arbitrary"), vmem_limit_bytes=VMEM
        ),
        interpret=interpret,
    )(lat, cb, lt, w)


def _grad_kernel(lat_ref, cb_ref, lt_ref, rowc_ref, tgt_ref, hw_ref, *refs, tm, tn, carry):
    if carry:
        prev_ref, tok_ref, cbg_ref = refs
    else:
        tok_ref, cbg_ref = refs
    j = pl.program_id(0)
    i = pl.program_id(1)
    logits = _logits(lat_ref, cb_ref)
    probs = jnp.exp(logits - lt_ref[...])
    cols = j * tn + lax.broadcasted_iota(jnp.int32, logits.shape, 1)
    hit = (cols == tgt_ref[...]).astype(jnp.float32)
    grad = (probs * (rowc_ref[...] + hw_ref[...] - 0.5 * logits) - hit).astype(jnp.bfloat16)
    tok = jnp.dot(grad, cb_ref[...], preferred_element_type=jnp.float32)
    cbg = lax.dot_general(
        grad, lat_ref[...], (((0,), (0,)), ((), ())), preferred_element_type=jnp.float32
    )
    rows = pl.ds(pl.multiple_of(i * tm, tm), tm)

    @pl.when(j == 0)
    def _():
        tok_ref[rows, :] = tok

    @pl.when(j > 0)
    def _():
        tok_ref[rows, :] = tok_ref[rows, :] + tok

    @pl.when(i == 0)
    def _():
        cbg_ref[...] = prev_ref[...] + cbg if carry else cbg

    @pl.when(i > 0)
    def _():
        cbg_ref[...] = cbg_ref[...] + cbg


def grads(lat, cb, lt, rowc, tgt, hw, prev=None, interpret=False):
    t_all, d = lat.shape
    s_all = cb.shape[0]
    tm, tn = min(TM, t_all), min(TN, s_all)
    row = pl.BlockSpec((tm, 1), lambda j, i: (i, 0))
    return pl.pallas_call(
        functools.partial(_grad_kernel, tm=tm, tn=tn, carry=prev is not None),
        grid=(s_all // tn, t_all // tm),
        in_specs=[
            pl.BlockSpec((tm, d), lambda j, i: (i, 0)),
            pl.BlockSpec((tn, d), lambda j, i: (j, 0)),
            row,
            row,
            row,
            pl.BlockSpec((1, tn), lambda j, i: (0, j)),
        ] + ([] if prev is None else [pl.BlockSpec((tn, d), lambda j, i: (j, 0))]),
        out_specs=[
            pl.BlockSpec((t_all, d), lambda j, i: (0, 0)),
            pl.BlockSpec((tn, d), lambda j, i: (j, 0)),
        ],
        out_shape=[
            jax.ShapeDtypeStruct((t_all, d), jnp.float32),
            jax.ShapeDtypeStruct((s_all, d), jnp.float32),
        ],
        compiler_params=pltpu.CompilerParams(
            dimension_semantics=("arbitrary", "arbitrary"), vmem_limit_bytes=VMEM
        ),
        input_output_aliases={} if prev is None else {6: 1},
        interpret=interpret,
    )(lat, cb, lt, rowc, tgt, hw, *([] if prev is None else [prev]))


def butterfly(values, axis, count, combine):
    step = 1
    while step < count:
        pairs = [(i, i ^ step) for i in range(count)]
        values = combine(values, lax.ppermute(values, axis, pairs))
        step *= 2
    return values


def butterfly_gather(block, axis, count):
    index = lax.axis_index(axis)
    step = 1
    while step < count:
        pairs = [(i, i ^ step) for i in range(count)]
        other = lax.ppermute(block, axis, pairs)
        low = (index // step) % 2 == 0
        block = jnp.where(low, jnp.concatenate([block, other]), jnp.concatenate([other, block]))
        step *= 2
    return block


def softmax_merge(a, b):
    top = jnp.maximum(a[0], b[0])
    wa = jnp.exp(a[0] - top)
    wb = jnp.exp(b[0] - top)
    return jnp.stack([top, a[1] * wa + b[1] * wb, a[2] * wa + b[2] * wb])


def is_pow2(n):
    return n & (n - 1) == 0


def rotate(latent, code_vec, cotangent):
    latent_norm = jnp.sqrt(jnp.sum(latent * latent, axis=1, keepdims=True) + norm_eps)
    code_norm = jnp.sqrt(jnp.sum(code_vec * code_vec, axis=1, keepdims=True) + norm_eps)
    latent_dir = latent / latent_norm
    code_dir = code_vec / code_norm
    cosine = jnp.sum(latent_dir * code_dir, axis=1, keepdims=True)
    summed = latent_dir + code_dir
    along = jnp.sum(summed * cotangent, axis=1, keepdims=True)
    facing = jnp.sum(code_dir * cotangent, axis=1, keepdims=True)
    turned = (
        cotangent
        - summed * along / jnp.maximum(1.0 + cosine, cos_floor)
        + 2.0 * latent_dir * facing
    )
    return code_norm / latent_norm * turned


def local(latents, codebook, hard_code, upstream):
    n_dp = lax.axis_size("dp")
    n_code = lax.axis_size("code")
    n_all = n_dp * n_code
    dp_i = lax.axis_index("dp")
    code_i = lax.axis_index("code")
    row_count = latents.shape[0]
    code_count = codebook.shape[0]
    width = latents.shape[1]
    tokens_total = row_count * n_dp
    slab = code_count // n_dp
    owned = row_count // n_code
    all_lat = lax.all_gather(latents, "dp", tiled=True)
    if is_pow2(n_dp):
        all_hard = butterfly_gather(hard_code, "dp", n_dp)
    else:
        all_hard = lax.all_gather(hard_code, "dp", tiled=True)
    my_codes = lax.dynamic_slice_in_dim(codebook, dp_i * slab, slab, axis=0)
    offset = code_i * code_count + dp_i * slab

    shard_target = hard_code - code_i * code_count
    holder = ((shard_target >= 0) & (shard_target < code_count))[:, None]
    picked_vec = jnp.where(
        holder, jnp.take(codebook, jnp.clip(shard_target, 0, code_count - 1), axis=0), 0
    ).astype(jnp.bfloat16)
    code_vec = lax.psum_scatter(picked_vec, "code", scatter_dimension=0, tiled=True).astype(jnp.float32)
    own_lat = lax.dynamic_slice_in_dim(latents, code_i * owned, owned, axis=0).astype(jnp.float32)
    own_up = lax.dynamic_slice_in_dim(upstream, code_i * owned, owned, axis=0).astype(jnp.float32)
    rotated = rotate(own_lat, code_vec, own_up)
    picked_sum = jnp.sum(LOGIT_SCALE * jnp.sum(own_lat * code_vec, axis=1))

    lane_top, lane_total, lane_moment = row_stats(all_lat, my_codes)
    local_top = jnp.max(lane_top, axis=1)
    lane_scale = jnp.exp(lane_top - local_top[:, None])
    stats = jnp.stack([
        local_top, jnp.sum(lane_total * lane_scale, axis=1), jnp.sum(lane_moment * lane_scale, axis=1)
    ])
    if is_pow2(n_all):
        row_top, row_total, moment = butterfly(stats, BOTH, n_all, softmax_merge)
    else:
        row_top = lax.pmax(stats[0], BOTH)
        scale = jnp.exp(stats[0] - row_top)
        row_total, moment = lax.psum((stats[1] * scale, stats[2] * scale), BOTH)
    log_total = row_top + jnp.log(row_total)
    mean_logit = moment / row_total
    entropy = log_total - mean_logit
    mean_usage = usage_sums(all_lat, my_codes, log_total[:, None])[0] / tokens_total
    log_usage = jnp.log(mean_usage + usage_eps)
    weight_term = log_usage + mean_usage / (mean_usage + usage_eps)
    spread_local = jnp.sum(spread_sums(all_lat, my_codes, log_total[:, None], weight_term[None, :]), axis=1)
    extras = jnp.stack([-jnp.sum(mean_usage * log_usage), picked_sum])
    joined = jnp.concatenate([spread_local, extras])
    if is_pow2(n_all):
        joined = butterfly(joined, BOTH, n_all, jnp.add)
    else:
        joined = lax.psum(joined, BOTH)
    spread, usage_entropy, picked_total = joined[:-2], joined[-2], joined[-1]

    row_coef = 1.0 + ENTROPY_WEIGHT * (mean_logit - spread)
    target = (all_hard - offset).astype(jnp.int32)
    token_acc, code_acc = grads(
        all_lat, my_codes, log_total[:, None], row_coef[:, None], target[:, None],
        ENTROPY_WEIGHT * weight_term[None, :],
    )
    token_parts = (LOGIT_SCALE * token_acc).astype(jnp.bfloat16).reshape(n_all, owned, width)
    token_parts = lax.all_to_all(token_parts, BOTH, 0, 0, tiled=False)
    token_sum = jnp.sum(token_parts.astype(jnp.float32), axis=0)
    codebook_grad = LOGIT_SCALE * code_acc
    token_grad = token_sum + rotated
    loss_terms = jnp.stack([
        (jnp.sum(log_total) - picked_total) / tokens_total,
        jnp.sum(entropy) / tokens_total,
        usage_entropy,
    ])
    return (token_grad, codebook_grad, loss_terms)


def solution(mesh):
    placed = (P("dp", None), P("code", None), P("dp"), P("dp", None))
    return jax.shard_map(
        local,
        mesh=mesh,
        in_specs=placed,
        out_specs=(P(("dp", "code"), None), P(("code", "dp"), None), P()),
        check_vma=False,
    )
```

```python
import jax
import jax.numpy as jnp
from jax import lax
from jax.experimental import pallas as pl
from jax.experimental.pallas import tpu as pltpu
from jax.sharding import PartitionSpec as P
import functools

LOGIT_SCALE = 5.0
ENTROPY_WEIGHT = 0.5
usage_eps = 1e-06
norm_eps = 1e-06
cos_floor = 0.25
BOTH = ("dp", "code")
TM = 512
TN = 2048
VMEM = 48 * 1024 * 1024


def _logits(lat_ref, cb_ref):
    return LOGIT_SCALE * lax.dot_general(
        lat_ref[...], cb_ref[...], (((1,), (1,)), ((), ())), preferred_element_type=jnp.float32
    )


def _lane_groups(x):
    return [x[:, g * 128:(g + 1) * 128] for g in range(x.shape[1] // 128)]


def _stats_kernel(lat_ref, cb_ref, m_ref, s_ref, t_ref):
    j = pl.program_id(1)

    @pl.when(j == 0)
    def _():
        m_ref[...] = jnp.full(m_ref.shape, -jnp.inf, jnp.float32)
        s_ref[...] = jnp.zeros(s_ref.shape, jnp.float32)
        t_ref[...] = jnp.zeros(t_ref.shape, jnp.float32)

    groups = _lane_groups(_logits(lat_ref, cb_ref))
    m_old = m_ref[...]
    m_new = functools.reduce(jnp.maximum, groups, m_old)
    rescale = jnp.exp(m_old - m_new)
    s_acc = s_ref[...] * rescale
    t_acc = t_ref[...] * rescale
    for g in groups:
        e = jnp.exp(g - m_new)
        s_acc = s_acc + e
        t_acc = t_acc + e * g
    m_ref[...] = m_new
    s_ref[...] = s_acc
    t_ref[...] = t_acc


def row_stats(lat, cb, interpret=False):
    t_all, d = lat.shape
    s_all = cb.shape[0]
    tm, tn = min(TM, t_all), min(TN, s_all)
    row = pl.BlockSpec((tm, 128), lambda i, j: (i, 0))
    lanes = jax.ShapeDtypeStruct((t_all, 128), jnp.float32)
    return pl.pallas_call(
        _stats_kernel,
        grid=(t_all // tm, s_all // tn),
        in_specs=[
            pl.BlockSpec((tm, d), lambda i, j: (i, 0)),
            pl.BlockSpec((tn, d), lambda i, j: (j, 0)),
        ],
        out_specs=[row, row, row],
        out_shape=[lanes] * 3,
        compiler_params=pltpu.CompilerParams(
            dimension_semantics=("arbitrary", "arbitrary"), vmem_limit_bytes=VMEM
        ),
        interpret=interpret,
    )(lat, cb)


def _usage_kernel(lat_ref, cb_ref, lt_ref, out_ref):
    i = pl.program_id(1)
    probs = jnp.exp(_logits(lat_ref, cb_ref) - lt_ref[:, 0:1])
    col = jnp.sum(probs, axis=0, keepdims=True)

    @pl.when(i == 0)
    def _():
        out_ref[...] = col

    @pl.when(i > 0)
    def _():
        out_ref[...] = out_ref[...] + col


def usage_sums(lat, cb, lt, interpret=False):
    t_all, d = lat.shape
    s_all = cb.shape[0]
    tm, tn = min(TM, t_all), min(TN, s_all)
    return pl.pallas_call(
        _usage_kernel,
        grid=(s_all // tn, t_all // tm),
        in_specs=[
            pl.BlockSpec((tm, d), lambda j, i: (i, 0)),
            pl.BlockSpec((tn, d), lambda j, i: (j, 0)),
            pl.BlockSpec((tm, 128), lambda j, i: (i, 0)),
        ],
        out_specs=pl.BlockSpec((1, tn), lambda j, i: (0, j)),
        out_shape=jax.ShapeDtypeStruct((1, s_all), jnp.float32),
        compiler_params=pltpu.CompilerParams(
            dimension_semantics=("arbitrary", "arbitrary"), vmem_limit_bytes=VMEM
        ),
        interpret=interpret,
    )(lat, cb, lt)


def _spread_kernel(lat_ref, cb_ref, lt_ref, w_ref, out_ref):
    j = pl.program_id(1)
    groups = _lane_groups(jnp.exp(_logits(lat_ref, cb_ref) - lt_ref[:, 0:1]))
    weights = _lane_groups(w_ref[...])
    part = groups[0] * weights[0]
    for g, w in zip(groups[1:], weights[1:]):
        part = part + g * w

    @pl.when(j == 0)
    def _():
        out_ref[...] = part

    @pl.when(j > 0)
    def _():
        out_ref[...] = out_ref[...] + part


def spread_sums(lat, cb, lt, w, interpret=False):
    t_all, d = lat.shape
    s_all = cb.shape[0]
    tm, tn = min(TM, t_all), min(TN, s_all)
    return pl.pallas_call(
        _spread_kernel,
        grid=(t_all // tm, s_all // tn),
        in_specs=[
            pl.BlockSpec((tm, d), lambda i, j: (i, 0)),
            pl.BlockSpec((tn, d), lambda i, j: (j, 0)),
            pl.BlockSpec((tm, 128), lambda i, j: (i, 0)),
            pl.BlockSpec((1, tn), lambda i, j: (0, j)),
        ],
        out_specs=pl.BlockSpec((tm, 128), lambda i, j: (i, 0)),
        out_shape=jax.ShapeDtypeStruct((t_all, 128), jnp.float32),
        compiler_params=pltpu.CompilerParams(
            dimension_semantics=("arbitrary", "arbitrary"), vmem_limit_bytes=VMEM
        ),
        interpret=interpret,
    )(lat, cb, lt, w)


def _grad_kernel(lat_ref, cb_ref, lt_ref, rowc_ref, tgt_ref, hw_ref, *refs, tm, tn, carry):
    if carry:
        prev_ref, tok_ref, cbg_ref = refs
    else:
        tok_ref, cbg_ref = refs
    j = pl.program_id(0)
    i = pl.program_id(1)
    logits = _logits(lat_ref, cb_ref)
    probs = jnp.exp(logits - lt_ref[:, 0:1])
    cols = j * tn + lax.broadcasted_iota(jnp.int32, logits.shape, 1)
    hit = (cols == tgt_ref[:, 0:1]).astype(jnp.float32)
    grad = (probs * (rowc_ref[:, 0:1] + hw_ref[...] - 0.5 * logits) - hit).astype(jnp.bfloat16)
    tok = jnp.dot(grad, cb_ref[...], preferred_element_type=jnp.float32)
    cbg = lax.dot_general(
        grad, lat_ref[...], (((0,), (0,)), ((), ())), preferred_element_type=jnp.float32
    )
    rows = pl.ds(pl.multiple_of(i * tm, tm), tm)

    @pl.when(j == 0)
    def _():
        tok_ref[rows, :] = tok

    @pl.when(j > 0)
    def _():
        tok_ref[rows, :] = tok_ref[rows, :] + tok

    @pl.when(i == 0)
    def _():
        cbg_ref[...] = prev_ref[...] + cbg if carry else cbg

    @pl.when(i > 0)
    def _():
        cbg_ref[...] = cbg_ref[...] + cbg


def grads(lat, cb, lt, rowc, tgt, hw, prev=None, interpret=False):
    t_all, d = lat.shape
    s_all = cb.shape[0]
    tm, tn = min(TM, t_all), min(TN, s_all)
    row = pl.BlockSpec((tm, 128), lambda j, i: (i, 0))
    return pl.pallas_call(
        functools.partial(_grad_kernel, tm=tm, tn=tn, carry=prev is not None),
        grid=(s_all // tn, t_all // tm),
        in_specs=[
            pl.BlockSpec((tm, d), lambda j, i: (i, 0)),
            pl.BlockSpec((tn, d), lambda j, i: (j, 0)),
            row,
            row,
            row,
            pl.BlockSpec((1, tn), lambda j, i: (0, j)),
        ] + ([] if prev is None else [pl.BlockSpec((tn, d), lambda j, i: (j, 0))]),
        out_specs=[
            pl.BlockSpec((t_all, d), lambda j, i: (0, 0)),
            pl.BlockSpec((tn, d), lambda j, i: (j, 0)),
        ],
        out_shape=[
            jax.ShapeDtypeStruct((t_all, d), jnp.float32),
            jax.ShapeDtypeStruct((s_all, d), jnp.float32),
        ],
        compiler_params=pltpu.CompilerParams(
            dimension_semantics=("arbitrary", "arbitrary"), vmem_limit_bytes=VMEM
        ),
        input_output_aliases={} if prev is None else {6: 1},
        interpret=interpret,
    )(lat, cb, lt, rowc, tgt, hw, *([] if prev is None else [prev]))


def butterfly(values, axis, count, combine):
    step = 1
    while step < count:
        pairs = [(i, i ^ step) for i in range(count)]
        values = combine(values, lax.ppermute(values, axis, pairs))
        step *= 2
    return values


def butterfly_gather(block, axis, count):
    index = lax.axis_index(axis)
    step = 1
    while step < count:
        pairs = [(i, i ^ step) for i in range(count)]
        other = lax.ppermute(block, axis, pairs)
        low = (index // step) % 2 == 0
        block = jnp.where(low, jnp.concatenate([block, other]), jnp.concatenate([other, block]))
        step *= 2
    return block


def softmax_merge(a, b):
    top = jnp.maximum(a[0], b[0])
    wa = jnp.exp(a[0] - top)
    wb = jnp.exp(b[0] - top)
    return jnp.stack([top, a[1] * wa + b[1] * wb, a[2] * wa + b[2] * wb])


def lanes(row_values):
    return jnp.broadcast_to(row_values[:, None], (row_values.shape[0], 128))


def is_pow2(n):
    return n & (n - 1) == 0


def rotate(latent, code_vec, cotangent):
    latent_norm = jnp.sqrt(jnp.sum(latent * latent, axis=1, keepdims=True) + norm_eps)
    code_norm = jnp.sqrt(jnp.sum(code_vec * code_vec, axis=1, keepdims=True) + norm_eps)
    latent_dir = latent / latent_norm
    code_dir = code_vec / code_norm
    cosine = jnp.sum(latent_dir * code_dir, axis=1, keepdims=True)
    summed = latent_dir + code_dir
    along = jnp.sum(summed * cotangent, axis=1, keepdims=True)
    facing = jnp.sum(code_dir * cotangent, axis=1, keepdims=True)
    turned = (
        cotangent
        - summed * along / jnp.maximum(1.0 + cosine, cos_floor)
        + 2.0 * latent_dir * facing
    )
    return code_norm / latent_norm * turned


def local(latents, codebook, hard_code, upstream):
    n_dp = lax.axis_size("dp")
    n_code = lax.axis_size("code")
    n_all = n_dp * n_code
    dp_i = lax.axis_index("dp")
    code_i = lax.axis_index("code")
    row_count = latents.shape[0]
    code_count = codebook.shape[0]
    width = latents.shape[1]
    tokens_total = row_count * n_dp
    slab = code_count // n_dp
    owned = row_count // n_code
    if is_pow2(n_dp):
        all_lat = butterfly_gather(latents, "dp", n_dp)
        all_hard = butterfly_gather(hard_code, "dp", n_dp)
    else:
        all_lat = lax.all_gather(latents, "dp", tiled=True)
        all_hard = lax.all_gather(hard_code, "dp", tiled=True)
    my_codes = lax.dynamic_slice_in_dim(codebook, dp_i * slab, slab, axis=0)
    offset = code_i * code_count + dp_i * slab

    shard_target = hard_code - code_i * code_count
    holder = ((shard_target >= 0) & (shard_target < code_count))[:, None]
    picked_vec = jnp.where(
        holder, jnp.take(codebook, jnp.clip(shard_target, 0, code_count - 1), axis=0), 0
    ).astype(jnp.bfloat16)
    code_vec = lax.psum_scatter(picked_vec, "code", scatter_dimension=0, tiled=True).astype(jnp.float32)
    own_lat = lax.dynamic_slice_in_dim(latents, code_i * owned, owned, axis=0).astype(jnp.float32)
    own_up = lax.dynamic_slice_in_dim(upstream, code_i * owned, owned, axis=0).astype(jnp.float32)
    rotated = rotate(own_lat, code_vec, own_up)
    picked_sum = jnp.sum(LOGIT_SCALE * jnp.sum(own_lat * code_vec, axis=1))

    lane_top, lane_total, lane_moment = row_stats(all_lat, my_codes)
    local_top = jnp.max(lane_top, axis=1)
    lane_scale = jnp.exp(lane_top - local_top[:, None])
    stats = jnp.stack([
        local_top, jnp.sum(lane_total * lane_scale, axis=1), jnp.sum(lane_moment * lane_scale, axis=1)
    ])
    if is_pow2(n_all):
        row_top, row_total, moment = butterfly(stats, BOTH, n_all, softmax_merge)
    else:
        row_top = lax.pmax(stats[0], BOTH)
        scale = jnp.exp(stats[0] - row_top)
        row_total, moment = lax.psum((stats[1] * scale, stats[2] * scale), BOTH)
    log_total = row_top + jnp.log(row_total)
    mean_logit = moment / row_total
    entropy = log_total - mean_logit
    mean_usage = usage_sums(all_lat, my_codes, lanes(log_total))[0] / tokens_total
    log_usage = jnp.log(mean_usage + usage_eps)
    weight_term = log_usage + mean_usage / (mean_usage + usage_eps)
    spread_local = jnp.sum(spread_sums(all_lat, my_codes, lanes(log_total), weight_term[None, :]), axis=1)
    extras = jnp.stack([-jnp.sum(mean_usage * log_usage), picked_sum])
    joined = jnp.concatenate([spread_local, extras])
    if is_pow2(n_all):
        joined = butterfly(joined, BOTH, n_all, jnp.add)
    else:
        joined = lax.psum(joined, BOTH)
    spread, usage_entropy, picked_total = joined[:-2], joined[-2], joined[-1]

    row_coef = 1.0 + ENTROPY_WEIGHT * (mean_logit - spread)
    target = (all_hard - offset).astype(jnp.int32)
    chunks = 2 if owned % 2 == 0 and (tokens_total // 2) % min(TM, tokens_total // 2) == 0 else 1
    piece = owned // chunks

    def reorder(x):
        x = x.reshape((n_all, chunks, piece) + x.shape[1:])
        return jnp.swapaxes(x, 0, 1).reshape((chunks, n_all * piece) + x.shape[3:])

    lat_c, lt_c, coef_c, tgt_c = (
        reorder(v) for v in (all_lat, lanes(log_total), lanes(row_coef), lanes(target))
    )
    half_weight = ENTROPY_WEIGHT * weight_term[None, :]
    code_acc = None
    parts = []
    for q in range(chunks):
        token_acc, code_acc = grads(
            lat_c[q], my_codes, lt_c[q], coef_c[q], tgt_c[q], half_weight, prev=code_acc
        )
        token_acc = (LOGIT_SCALE * token_acc).astype(jnp.bfloat16).reshape(n_all, piece, width)
        token_acc = lax.all_to_all(token_acc, BOTH, 0, 0, tiled=False)
        parts.append(jnp.sum(token_acc.astype(jnp.float32), axis=0))
    token_sum = jnp.concatenate(parts, axis=0)
    codebook_grad = LOGIT_SCALE * code_acc
    token_grad = token_sum + rotated
    loss_terms = jnp.stack([
        (jnp.sum(log_total) - picked_total) / tokens_total,
        jnp.sum(entropy) / tokens_total,
        usage_entropy,
    ])
    return (token_grad, codebook_grad, loss_terms)


def solution(mesh):
    placed = (P("dp", None), P("code", None), P("dp"), P("dp", None))
    return jax.shard_map(
        local,
        mesh=mesh,
        in_specs=placed,
        out_specs=(P(("dp", "code"), None), P(("code", "dp"), None), P()),
        check_vma=False,
    )
```

```python
import jax
import jax.numpy as jnp
from jax import lax
from jax.experimental import pallas as pl
from jax.experimental.pallas import tpu as pltpu
from jax.sharding import PartitionSpec as P
import functools

LOGIT_SCALE = 5.0
ENTROPY_WEIGHT = 0.5
usage_eps = 1e-06
norm_eps = 1e-06
cos_floor = 0.25
BOTH = ("dp", "code")
TM = 512
TN = 2048
VMEM = 48 * 1024 * 1024


def _logits(lat_ref, cb_ref):
    return LOGIT_SCALE * lax.dot_general(
        lat_ref[...], cb_ref[...], (((1,), (1,)), ((), ())), preferred_element_type=jnp.float32
    )


def _lane_groups(x):
    return [x[:, g * 128:(g + 1) * 128] for g in range(x.shape[1] // 128)]


def _stats_kernel(lat_ref, cb_ref, m_ref, s_ref, t_ref):
    j = pl.program_id(1)

    @pl.when(j == 0)
    def _():
        m_ref[...] = jnp.full(m_ref.shape, -jnp.inf, jnp.float32)
        s_ref[...] = jnp.zeros(s_ref.shape, jnp.float32)
        t_ref[...] = jnp.zeros(t_ref.shape, jnp.float32)

    groups = _lane_groups(_logits(lat_ref, cb_ref))
    m_old = m_ref[...]
    m_new = functools.reduce(jnp.maximum, groups, m_old)
    rescale = jnp.exp(m_old - m_new)
    s_acc = s_ref[...] * rescale
    t_acc = t_ref[...] * rescale
    for g in groups:
        e = jnp.exp(g - m_new)
        s_acc = s_acc + e
        t_acc = t_acc + e * g
    m_ref[...] = m_new
    s_ref[...] = s_acc
    t_ref[...] = t_acc


def row_stats(lat, cb, interpret=False):
    t_all, d = lat.shape
    s_all = cb.shape[0]
    tm, tn = min(TM, t_all), min(TN, s_all)
    row = pl.BlockSpec((tm, 128), lambda i, j: (i, 0))
    lanes = jax.ShapeDtypeStruct((t_all, 128), jnp.float32)
    return pl.pallas_call(
        _stats_kernel,
        grid=(t_all // tm, s_all // tn),
        in_specs=[
            pl.BlockSpec((tm, d), lambda i, j: (i, 0)),
            pl.BlockSpec((tn, d), lambda i, j: (j, 0)),
        ],
        out_specs=[row, row, row],
        out_shape=[lanes] * 3,
        compiler_params=pltpu.CompilerParams(
            dimension_semantics=("arbitrary", "arbitrary"), vmem_limit_bytes=VMEM
        ),
        interpret=interpret,
    )(lat, cb)


def _usage_kernel(lat_ref, cb_ref, lt_ref, out_ref):
    i = pl.program_id(1)
    probs = jnp.exp(_logits(lat_ref, cb_ref) - lt_ref[:, 0:1])
    col = jnp.sum(probs, axis=0, keepdims=True)

    @pl.when(i == 0)
    def _():
        out_ref[...] = col

    @pl.when(i > 0)
    def _():
        out_ref[...] = out_ref[...] + col


def usage_sums(lat, cb, lt, interpret=False):
    t_all, d = lat.shape
    s_all = cb.shape[0]
    tm, tn = min(TM, t_all), min(TN, s_all)
    return pl.pallas_call(
        _usage_kernel,
        grid=(s_all // tn, t_all // tm),
        in_specs=[
            pl.BlockSpec((tm, d), lambda j, i: (i, 0)),
            pl.BlockSpec((tn, d), lambda j, i: (j, 0)),
            pl.BlockSpec((tm, 128), lambda j, i: (i, 0)),
        ],
        out_specs=pl.BlockSpec((1, tn), lambda j, i: (0, j)),
        out_shape=jax.ShapeDtypeStruct((1, s_all), jnp.float32),
        compiler_params=pltpu.CompilerParams(
            dimension_semantics=("arbitrary", "arbitrary"), vmem_limit_bytes=VMEM
        ),
        interpret=interpret,
    )(lat, cb, lt)


def _spread_kernel(lat_ref, cb_ref, lt_ref, w_ref, out_ref):
    j = pl.program_id(1)
    groups = _lane_groups(jnp.exp(_logits(lat_ref, cb_ref) - lt_ref[:, 0:1]))
    weights = _lane_groups(w_ref[...])
    part = groups[0] * weights[0]
    for g, w in zip(groups[1:], weights[1:]):
        part = part + g * w

    @pl.when(j == 0)
    def _():
        out_ref[...] = part

    @pl.when(j > 0)
    def _():
        out_ref[...] = out_ref[...] + part


def spread_sums(lat, cb, lt, w, interpret=False):
    t_all, d = lat.shape
    s_all = cb.shape[0]
    tm, tn = min(TM, t_all), min(TN, s_all)
    return pl.pallas_call(
        _spread_kernel,
        grid=(t_all // tm, s_all // tn),
        in_specs=[
            pl.BlockSpec((tm, d), lambda i, j: (i, 0)),
            pl.BlockSpec((tn, d), lambda i, j: (j, 0)),
            pl.BlockSpec((tm, 128), lambda i, j: (i, 0)),
            pl.BlockSpec((1, tn), lambda i, j: (0, j)),
        ],
        out_specs=pl.BlockSpec((tm, 128), lambda i, j: (i, 0)),
        out_shape=jax.ShapeDtypeStruct((t_all, 128), jnp.float32),
        compiler_params=pltpu.CompilerParams(
            dimension_semantics=("arbitrary", "arbitrary"), vmem_limit_bytes=VMEM
        ),
        interpret=interpret,
    )(lat, cb, lt, w)


def _grad_kernel(lat_ref, cb_ref, lt_ref, rowc_ref, tgt_ref, hw_ref, *refs, tm, tn, carry):
    if carry:
        prev_ref, tok_ref, cbg_ref = refs
    else:
        tok_ref, cbg_ref = refs
    j = pl.program_id(0)
    i = pl.program_id(1)
    logits = _logits(lat_ref, cb_ref)
    probs = jnp.exp(logits - lt_ref[:, 0:1])
    cols = lax.broadcasted_iota(jnp.int32, logits.shape, 1)
    hit = cols == tgt_ref[:, 0:1] - j * tn
    grad = probs * (rowc_ref[:, 0:1] + hw_ref[...] - 0.5 * logits)
    grad = jnp.where(hit, grad - 1.0, grad).astype(jnp.bfloat16)
    tok = jnp.dot(grad, cb_ref[...], preferred_element_type=jnp.float32)
    cbg = lax.dot_general(
        grad, lat_ref[...], (((0,), (0,)), ((), ())), preferred_element_type=jnp.float32
    )
    rows = pl.ds(pl.multiple_of(i * tm, tm), tm)

    @pl.when(j == 0)
    def _():
        tok_ref[rows, :] = tok

    @pl.when(j > 0)
    def _():
        tok_ref[rows, :] = tok_ref[rows, :] + tok

    @pl.when(i == 0)
    def _():
        cbg_ref[...] = prev_ref[...] + cbg if carry else cbg

    @pl.when(i > 0)
    def _():
        cbg_ref[...] = cbg_ref[...] + cbg


def grads(lat, cb, lt, rowc, tgt, hw, prev=None, interpret=False):
    t_all, d = lat.shape
    s_all = cb.shape[0]
    tm, tn = min(TM, t_all), min(TN, s_all)
    row = pl.BlockSpec((tm, 128), lambda j, i: (i, 0))
    return pl.pallas_call(
        functools.partial(_grad_kernel, tm=tm, tn=tn, carry=prev is not None),
        grid=(s_all // tn, t_all // tm),
        in_specs=[
            pl.BlockSpec((tm, d), lambda j, i: (i, 0)),
            pl.BlockSpec((tn, d), lambda j, i: (j, 0)),
            row,
            row,
            row,
            pl.BlockSpec((1, tn), lambda j, i: (0, j)),
        ] + ([] if prev is None else [pl.BlockSpec((tn, d), lambda j, i: (j, 0))]),
        out_specs=[
            pl.BlockSpec((t_all, d), lambda j, i: (0, 0)),
            pl.BlockSpec((tn, d), lambda j, i: (j, 0)),
        ],
        out_shape=[
            jax.ShapeDtypeStruct((t_all, d), jnp.float32),
            jax.ShapeDtypeStruct((s_all, d), jnp.float32),
        ],
        compiler_params=pltpu.CompilerParams(
            dimension_semantics=("arbitrary", "arbitrary"), vmem_limit_bytes=VMEM
        ),
        input_output_aliases={} if prev is None else {6: 1},
        interpret=interpret,
    )(lat, cb, lt, rowc, tgt, hw, *([] if prev is None else [prev]))


def butterfly(values, axis, count, combine):
    step = 1
    while step < count:
        pairs = [(i, i ^ step) for i in range(count)]
        values = combine(values, lax.ppermute(values, axis, pairs))
        step *= 2
    return values


def butterfly_gather(block, axis, count):
    index = lax.axis_index(axis)
    step = 1
    while step < count:
        pairs = [(i, i ^ step) for i in range(count)]
        other = lax.ppermute(block, axis, pairs)
        low = (index // step) % 2 == 0
        block = jnp.where(low, jnp.concatenate([block, other]), jnp.concatenate([other, block]))
        step *= 2
    return block


def softmax_merge(a, b):
    top = jnp.maximum(a[0], b[0])
    wa = jnp.exp(a[0] - top)
    wb = jnp.exp(b[0] - top)
    return jnp.stack([top, a[1] * wa + b[1] * wb, a[2] * wa + b[2] * wb])


def lanes(row_values):
    return jnp.broadcast_to(row_values[:, None], (row_values.shape[0], 128))


def is_pow2(n):
    return n & (n - 1) == 0


def rotate(latent, code_vec, cotangent):
    latent_norm = jnp.sqrt(jnp.sum(latent * latent, axis=1, keepdims=True) + norm_eps)
    code_norm = jnp.sqrt(jnp.sum(code_vec * code_vec, axis=1, keepdims=True) + norm_eps)
    latent_dir = latent / latent_norm
    code_dir = code_vec / code_norm
    cosine = jnp.sum(latent_dir * code_dir, axis=1, keepdims=True)
    summed = latent_dir + code_dir
    along = jnp.sum(summed * cotangent, axis=1, keepdims=True)
    facing = jnp.sum(code_dir * cotangent, axis=1, keepdims=True)
    turned = (
        cotangent
        - summed * along / jnp.maximum(1.0 + cosine, cos_floor)
        + 2.0 * latent_dir * facing
    )
    return code_norm / latent_norm * turned


def local(latents, codebook, hard_code, upstream):
    n_dp = lax.axis_size("dp")
    n_code = lax.axis_size("code")
    n_all = n_dp * n_code
    dp_i = lax.axis_index("dp")
    code_i = lax.axis_index("code")
    row_count = latents.shape[0]
    code_count = codebook.shape[0]
    width = latents.shape[1]
    tokens_total = row_count * n_dp
    slab = code_count // n_dp
    owned = row_count // n_code
    all_lat = lax.all_gather(latents, "dp", tiled=True)
    if is_pow2(n_dp):
        all_hard = butterfly_gather(hard_code, "dp", n_dp)
    else:
        all_hard = lax.all_gather(hard_code, "dp", tiled=True)
    my_codes = lax.dynamic_slice_in_dim(codebook, dp_i * slab, slab, axis=0)
    offset = code_i * code_count + dp_i * slab

    shard_target = hard_code - code_i * code_count
    holder = ((shard_target >= 0) & (shard_target < code_count))[:, None]
    picked_vec = jnp.where(
        holder, jnp.take(codebook, jnp.clip(shard_target, 0, code_count - 1), axis=0), 0
    ).astype(jnp.bfloat16)
    code_vec = lax.psum_scatter(picked_vec, "code", scatter_dimension=0, tiled=True).astype(jnp.float32)
    own_lat = lax.dynamic_slice_in_dim(latents, code_i * owned, owned, axis=0).astype(jnp.float32)
    own_up = lax.dynamic_slice_in_dim(upstream, code_i * owned, owned, axis=0).astype(jnp.float32)
    rotated = rotate(own_lat, code_vec, own_up)
    picked_sum = jnp.sum(LOGIT_SCALE * jnp.sum(own_lat * code_vec, axis=1))

    lane_top, lane_total, lane_moment = row_stats(latents, codebook)
    local_top = jnp.max(lane_top, axis=1)
    lane_scale = jnp.exp(lane_top - local_top[:, None])
    stats = jnp.stack([
        local_top, jnp.sum(lane_total * lane_scale, axis=1), jnp.sum(lane_moment * lane_scale, axis=1)
    ])
    if is_pow2(n_code):
        row_top, row_total, moment = butterfly(stats, "code", n_code, softmax_merge)
    else:
        row_top = lax.pmax(stats[0], "code")
        scale = jnp.exp(stats[0] - row_top)
        row_total, moment = lax.psum((stats[1] * scale, stats[2] * scale), "code")
    token_stats = jnp.stack([row_top + jnp.log(row_total), moment / row_total], axis=1)
    if is_pow2(n_dp):
        token_stats = butterfly_gather(token_stats, "dp", n_dp)
    else:
        token_stats = lax.all_gather(token_stats, "dp", tiled=True)
    log_total = token_stats[:, 0]
    mean_logit = token_stats[:, 1]
    entropy = log_total - mean_logit
    mean_usage = usage_sums(all_lat, my_codes, lanes(log_total))[0] / tokens_total
    log_usage = jnp.log(mean_usage + usage_eps)
    weight_term = log_usage + mean_usage / (mean_usage + usage_eps)
    spread_local = jnp.sum(spread_sums(all_lat, my_codes, lanes(log_total), weight_term[None, :]), axis=1)
    extras = jnp.stack([-jnp.sum(mean_usage * log_usage), picked_sum])
    joined = jnp.concatenate([spread_local, extras])
    if is_pow2(n_all):
        joined = butterfly(joined, BOTH, n_all, jnp.add)
    else:
        joined = lax.psum(joined, BOTH)
    spread, usage_entropy, picked_total = joined[:-2], joined[-2], joined[-1]

    row_coef = 1.0 + ENTROPY_WEIGHT * (mean_logit - spread)
    target = (all_hard - offset).astype(jnp.int32)
    chunks = 2 if owned % 2 == 0 and (tokens_total // 2) % min(TM, tokens_total // 2) == 0 else 1
    piece = owned // chunks

    def reorder(x):
        x = x.reshape((n_all, chunks, piece) + x.shape[1:])
        return jnp.swapaxes(x, 0, 1).reshape((chunks, n_all * piece) + x.shape[3:])

    lat_c, lt_c, coef_c, tgt_c = (
        reorder(v) for v in (all_lat, lanes(log_total), lanes(row_coef), lanes(target))
    )
    half_weight = ENTROPY_WEIGHT * weight_term[None, :]
    code_acc = None
    parts = []
    for q in range(chunks):
        token_acc, code_acc = grads(
            lat_c[q], my_codes, lt_c[q], coef_c[q], tgt_c[q], half_weight, prev=code_acc
        )
        token_acc = (LOGIT_SCALE * token_acc).astype(jnp.bfloat16).reshape(n_all, piece, width)
        token_acc = lax.all_to_all(token_acc, BOTH, 0, 0, tiled=False)
        parts.append(jnp.sum(token_acc.astype(jnp.float32), axis=0))
    token_sum = jnp.concatenate(parts, axis=0)
    codebook_grad = LOGIT_SCALE * code_acc
    token_grad = token_sum + rotated
    loss_terms = jnp.stack([
        (jnp.sum(log_total) - picked_total) / tokens_total,
        jnp.sum(entropy) / tokens_total,
        usage_entropy,
    ])
    return (token_grad, codebook_grad, loss_terms)


def solution(mesh):
    placed = (P("dp", None), P("code", None), P("dp"), P("dp", None))
    return jax.shard_map(
        local,
        mesh=mesh,
        in_specs=placed,
        out_specs=(P(("dp", "code"), None), P(("code", "dp"), None), P()),
        check_vma=False,
    )
```

```python
import jax
import jax.numpy as jnp
from jax import lax
from jax.experimental import pallas as pl
from jax.experimental.pallas import tpu as pltpu
from jax.sharding import PartitionSpec as P
import functools

LOGIT_SCALE = 5.0
ENTROPY_WEIGHT = 0.5
usage_eps = 1e-06
norm_eps = 1e-06
cos_floor = 0.25
BOTH = ("dp", "code")
TM = 512
TN = 2048
VMEM = 48 * 1024 * 1024


def _logits(lat_ref, cb_ref):
    return LOGIT_SCALE * lax.dot_general(
        lat_ref[...], cb_ref[...], (((1,), (1,)), ((), ())), preferred_element_type=jnp.float32
    )


def _lane_groups(x):
    return [x[:, g * 128:(g + 1) * 128] for g in range(x.shape[1] // 128)]


def _stats_kernel(lat_ref, cb_ref, m_ref, s_ref, t_ref):
    j = pl.program_id(1)

    @pl.when(j == 0)
    def _():
        m_ref[...] = jnp.full(m_ref.shape, -jnp.inf, jnp.float32)
        s_ref[...] = jnp.zeros(s_ref.shape, jnp.float32)
        t_ref[...] = jnp.zeros(t_ref.shape, jnp.float32)

    groups = _lane_groups(_logits(lat_ref, cb_ref))
    m_old = m_ref[...]
    m_new = functools.reduce(jnp.maximum, groups, m_old)
    rescale = jnp.exp(m_old - m_new)
    s_acc = s_ref[...] * rescale
    t_acc = t_ref[...] * rescale
    for g in groups:
        e = jnp.exp(g - m_new)
        s_acc = s_acc + e
        t_acc = t_acc + e * g
    m_ref[...] = m_new
    s_ref[...] = s_acc
    t_ref[...] = t_acc


def row_stats(lat, cb, interpret=False):
    t_all, d = lat.shape
    s_all = cb.shape[0]
    tm, tn = min(TM, t_all), min(TN, s_all)
    row = pl.BlockSpec((tm, 128), lambda i, j: (i, 0))
    lanes = jax.ShapeDtypeStruct((t_all, 128), jnp.float32)
    return pl.pallas_call(
        _stats_kernel,
        grid=(t_all // tm, s_all // tn),
        in_specs=[
            pl.BlockSpec((tm, d), lambda i, j: (i, 0)),
            pl.BlockSpec((tn, d), lambda i, j: (j, 0)),
        ],
        out_specs=[row, row, row],
        out_shape=[lanes] * 3,
        compiler_params=pltpu.CompilerParams(
            dimension_semantics=("arbitrary", "arbitrary"), vmem_limit_bytes=VMEM
        ),
        interpret=interpret,
    )(lat, cb)


def _usage_kernel(lat_ref, cb_ref, lt_ref, out_ref):
    i = pl.program_id(1)
    probs = jnp.exp(_logits(lat_ref, cb_ref) - lt_ref[:, 0:1])
    col = jnp.sum(probs, axis=0, keepdims=True)

    @pl.when(i == 0)
    def _():
        out_ref[...] = col

    @pl.when(i > 0)
    def _():
        out_ref[...] = out_ref[...] + col


def usage_sums(lat, cb, lt, interpret=False):
    t_all, d = lat.shape
    s_all = cb.shape[0]
    tm, tn = min(TM, t_all), min(TN, s_all)
    return pl.pallas_call(
        _usage_kernel,
        grid=(s_all // tn, t_all // tm),
        in_specs=[
            pl.BlockSpec((tm, d), lambda j, i: (i, 0)),
            pl.BlockSpec((tn, d), lambda j, i: (j, 0)),
            pl.BlockSpec((tm, 128), lambda j, i: (i, 0)),
        ],
        out_specs=pl.BlockSpec((1, tn), lambda j, i: (0, j)),
        out_shape=jax.ShapeDtypeStruct((1, s_all), jnp.float32),
        compiler_params=pltpu.CompilerParams(
            dimension_semantics=("arbitrary", "arbitrary"), vmem_limit_bytes=VMEM
        ),
        interpret=interpret,
    )(lat, cb, lt)


def _spread_kernel(lat_ref, cb_ref, lt_ref, w_ref, out_ref):
    j = pl.program_id(1)
    groups = _lane_groups(jnp.exp(_logits(lat_ref, cb_ref) - lt_ref[:, 0:1]))
    weights = _lane_groups(w_ref[...])
    part = groups[0] * weights[0]
    for g, w in zip(groups[1:], weights[1:]):
        part = part + g * w

    @pl.when(j == 0)
    def _():
        out_ref[...] = part

    @pl.when(j > 0)
    def _():
        out_ref[...] = out_ref[...] + part


def spread_sums(lat, cb, lt, w, interpret=False):
    t_all, d = lat.shape
    s_all = cb.shape[0]
    tm, tn = min(TM, t_all), min(TN, s_all)
    return pl.pallas_call(
        _spread_kernel,
        grid=(t_all // tm, s_all // tn),
        in_specs=[
            pl.BlockSpec((tm, d), lambda i, j: (i, 0)),
            pl.BlockSpec((tn, d), lambda i, j: (j, 0)),
            pl.BlockSpec((tm, 128), lambda i, j: (i, 0)),
            pl.BlockSpec((1, tn), lambda i, j: (0, j)),
        ],
        out_specs=pl.BlockSpec((tm, 128), lambda i, j: (i, 0)),
        out_shape=jax.ShapeDtypeStruct((t_all, 128), jnp.float32),
        compiler_params=pltpu.CompilerParams(
            dimension_semantics=("arbitrary", "arbitrary"), vmem_limit_bytes=VMEM
        ),
        interpret=interpret,
    )(lat, cb, lt, w)


def _grad_kernel(lat_ref, cb_ref, lt_ref, rowc_ref, tgt_ref, hw_ref, *refs, tm, tn, carry):
    if carry:
        prev_ref, tok_ref, cbg_ref = refs
    else:
        tok_ref, cbg_ref = refs
    j = pl.program_id(0)
    i = pl.program_id(1)
    logits = _logits(lat_ref, cb_ref)
    probs = jnp.exp(logits - lt_ref[:, 0:1])
    cols = j * tn + lax.broadcasted_iota(jnp.int32, logits.shape, 1)
    hit = (cols == tgt_ref[:, 0:1]).astype(jnp.float32)
    grad = (probs * (rowc_ref[:, 0:1] + hw_ref[...] - 0.5 * logits) - hit).astype(jnp.bfloat16)
    tok = jnp.dot(grad, cb_ref[...], preferred_element_type=jnp.float32)
    cbg = lax.dot_general(
        grad, lat_ref[...], (((0,), (0,)), ((), ())), preferred_element_type=jnp.float32
    )
    rows = pl.ds(pl.multiple_of(i * tm, tm), tm)

    @pl.when(j == 0)
    def _():
        tok_ref[rows, :] = tok

    @pl.when(j > 0)
    def _():
        tok_ref[rows, :] = tok_ref[rows, :] + tok

    @pl.when(i == 0)
    def _():
        cbg_ref[...] = prev_ref[...] + cbg if carry else cbg

    @pl.when(i > 0)
    def _():
        cbg_ref[...] = cbg_ref[...] + cbg


def grads(lat, cb, lt, rowc, tgt, hw, prev=None, interpret=False):
    t_all, d = lat.shape
    s_all = cb.shape[0]
    tm, tn = min(TM, t_all), min(TN, s_all)
    row = pl.BlockSpec((tm, 128), lambda j, i: (i, 0))
    return pl.pallas_call(
        functools.partial(_grad_kernel, tm=tm, tn=tn, carry=prev is not None),
        grid=(s_all // tn, t_all // tm),
        in_specs=[
            pl.BlockSpec((tm, d), lambda j, i: (i, 0)),
            pl.BlockSpec((tn, d), lambda j, i: (j, 0)),
            row,
            row,
            row,
            pl.BlockSpec((1, tn), lambda j, i: (0, j)),
        ] + ([] if prev is None else [pl.BlockSpec((tn, d), lambda j, i: (j, 0))]),
        out_specs=[
            pl.BlockSpec((t_all, d), lambda j, i: (0, 0)),
            pl.BlockSpec((tn, d), lambda j, i: (j, 0)),
        ],
        out_shape=[
            jax.ShapeDtypeStruct((t_all, d), jnp.float32),
            jax.ShapeDtypeStruct((s_all, d), jnp.float32),
        ],
        compiler_params=pltpu.CompilerParams(
            dimension_semantics=("arbitrary", "arbitrary"), vmem_limit_bytes=VMEM
        ),
        input_output_aliases={} if prev is None else {6: 1},
        interpret=interpret,
    )(lat, cb, lt, rowc, tgt, hw, *([] if prev is None else [prev]))


def butterfly(values, axis, count, combine):
    step = 1
    while step < count:
        pairs = [(i, i ^ step) for i in range(count)]
        values = combine(values, lax.ppermute(values, axis, pairs))
        step *= 2
    return values


def butterfly_gather(block, axis, count):
    index = lax.axis_index(axis)
    step = 1
    while step < count:
        pairs = [(i, i ^ step) for i in range(count)]
        other = lax.ppermute(block, axis, pairs)
        low = (index // step) % 2 == 0
        block = jnp.where(low, jnp.concatenate([block, other]), jnp.concatenate([other, block]))
        step *= 2
    return block


def softmax_merge(a, b):
    top = jnp.maximum(a[0], b[0])
    wa = jnp.exp(a[0] - top)
    wb = jnp.exp(b[0] - top)
    return jnp.stack([top, a[1] * wa + b[1] * wb, a[2] * wa + b[2] * wb])


def lanes(row_values):
    return jnp.broadcast_to(row_values[:, None], (row_values.shape[0], 128))


def is_pow2(n):
    return n & (n - 1) == 0


def rotate(latent, code_vec, cotangent):
    latent_norm = jnp.sqrt(jnp.sum(latent * latent, axis=1, keepdims=True) + norm_eps)
    code_norm = jnp.sqrt(jnp.sum(code_vec * code_vec, axis=1, keepdims=True) + norm_eps)
    latent_dir = latent / latent_norm
    code_dir = code_vec / code_norm
    cosine = jnp.sum(latent_dir * code_dir, axis=1, keepdims=True)
    summed = latent_dir + code_dir
    along = jnp.sum(summed * cotangent, axis=1, keepdims=True)
    facing = jnp.sum(code_dir * cotangent, axis=1, keepdims=True)
    turned = (
        cotangent
        - summed * along / jnp.maximum(1.0 + cosine, cos_floor)
        + 2.0 * latent_dir * facing
    )
    return code_norm / latent_norm * turned


def local(latents, codebook, hard_code, upstream):
    n_dp = lax.axis_size("dp")
    n_code = lax.axis_size("code")
    n_all = n_dp * n_code
    dp_i = lax.axis_index("dp")
    code_i = lax.axis_index("code")
    row_count = latents.shape[0]
    code_count = codebook.shape[0]
    width = latents.shape[1]
    tokens_total = row_count * n_dp
    slab = code_count // n_dp
    owned = row_count // n_code
    all_lat = lax.all_gather(latents, "dp", tiled=True)
    if is_pow2(n_dp):
        all_hard = butterfly_gather(hard_code, "dp", n_dp)
    else:
        all_hard = lax.all_gather(hard_code, "dp", tiled=True)
    my_codes = lax.dynamic_slice_in_dim(codebook, dp_i * slab, slab, axis=0)
    offset = code_i * code_count + dp_i * slab

    lane_top, lane_total, lane_moment = row_stats(latents, codebook)
    shard_target = hard_code - code_i * code_count
    holder = ((shard_target >= 0) & (shard_target < code_count))[:, None]
    late_codebook, _ = lax.optimization_barrier((codebook, lane_top))
    picked_vec = jnp.where(
        holder, jnp.take(late_codebook, jnp.clip(shard_target, 0, code_count - 1), axis=0), 0
    ).astype(jnp.bfloat16)
    picked_vec = lax.all_to_all(picked_vec.reshape(n_code, owned, width), "code", 0, 0, tiled=False)
    code_vec = jnp.sum(picked_vec.astype(jnp.float32), axis=0)
    own_lat = lax.dynamic_slice_in_dim(latents, code_i * owned, owned, axis=0).astype(jnp.float32)
    own_up = lax.dynamic_slice_in_dim(upstream, code_i * owned, owned, axis=0).astype(jnp.float32)
    rotated = rotate(own_lat, code_vec, own_up)
    picked_sum = jnp.sum(LOGIT_SCALE * jnp.sum(own_lat * code_vec, axis=1))

    local_top = jnp.max(lane_top, axis=1)
    lane_scale = jnp.exp(lane_top - local_top[:, None])
    stats = jnp.stack([
        local_top, jnp.sum(lane_total * lane_scale, axis=1), jnp.sum(lane_moment * lane_scale, axis=1)
    ])
    if is_pow2(n_code):
        row_top, row_total, moment = butterfly(stats, "code", n_code, softmax_merge)
    else:
        row_top = lax.pmax(stats[0], "code")
        scale = jnp.exp(stats[0] - row_top)
        row_total, moment = lax.psum((stats[1] * scale, stats[2] * scale), "code")
    token_stats = jnp.stack([row_top + jnp.log(row_total), moment / row_total], axis=1)
    if is_pow2(n_dp):
        token_stats = butterfly_gather(token_stats, "dp", n_dp)
    else:
        token_stats = lax.all_gather(token_stats, "dp", tiled=True)
    log_total = token_stats[:, 0]
    mean_logit = token_stats[:, 1]
    entropy = log_total - mean_logit
    mean_usage = usage_sums(all_lat, my_codes, lanes(log_total))[0] / tokens_total
    log_usage = jnp.log(mean_usage + usage_eps)
    weight_term = log_usage + mean_usage / (mean_usage + usage_eps)
    spread_local = jnp.sum(spread_sums(all_lat, my_codes, lanes(log_total), weight_term[None, :]), axis=1)
    extras = jnp.stack([-jnp.sum(mean_usage * log_usage), picked_sum])
    joined = jnp.concatenate([spread_local, extras])
    if is_pow2(n_all):
        joined = butterfly(joined, BOTH, n_all, jnp.add)
    else:
        joined = lax.psum(joined, BOTH)
    spread, usage_entropy, picked_total = joined[:-2], joined[-2], joined[-1]

    row_coef = 1.0 + ENTROPY_WEIGHT * (mean_logit - spread)
    target = (all_hard - offset).astype(jnp.int32)
    chunks = 2 if owned % 2 == 0 and (tokens_total // 2) % min(TM, tokens_total // 2) == 0 else 1
    piece = owned // chunks

    def reorder(x):
        x = x.reshape((n_all, chunks, piece) + x.shape[1:])
        return jnp.swapaxes(x, 0, 1).reshape((chunks, n_all * piece) + x.shape[3:])

    lat_c, lt_c, coef_c, tgt_c = (
        reorder(v) for v in (all_lat, lanes(log_total), lanes(row_coef), lanes(target))
    )
    half_weight = ENTROPY_WEIGHT * weight_term[None, :]
    code_acc = None
    parts = []
    for q in range(chunks):
        token_acc, code_acc = grads(
            lat_c[q], my_codes, lt_c[q], coef_c[q], tgt_c[q], half_weight, prev=code_acc
        )
        token_acc = (LOGIT_SCALE * token_acc).astype(jnp.bfloat16).reshape(n_all, piece, width)
        token_acc = lax.all_to_all(token_acc, BOTH, 0, 0, tiled=False)
        parts.append(jnp.sum(token_acc.astype(jnp.float32), axis=0))
    token_sum = jnp.concatenate(parts, axis=0)
    codebook_grad = LOGIT_SCALE * code_acc
    token_grad = token_sum + rotated
    loss_terms = jnp.stack([
        (jnp.sum(log_total) - picked_total) / tokens_total,
        jnp.sum(entropy) / tokens_total,
        usage_entropy,
    ])
    return (token_grad, codebook_grad, loss_terms)


def solution(mesh):
    placed = (P("dp", None), P("code", None), P("dp"), P("dp", None))
    return jax.shard_map(
        local,
        mesh=mesh,
        in_specs=placed,
        out_specs=(P(("dp", "code"), None), P(("code", "dp"), None), P()),
        check_vma=False,
    )
```

```python
import jax
import jax.numpy as jnp
from jax import lax
from jax.experimental import pallas as pl
from jax.experimental.pallas import tpu as pltpu
from jax.sharding import PartitionSpec as P
import functools

LOGIT_SCALE = 5.0
ENTROPY_WEIGHT = 0.5
usage_eps = 1e-06
norm_eps = 1e-06
cos_floor = 0.25
BOTH = ("dp", "code")
TM = 512
TN = 4096
VMEM = 48 * 1024 * 1024


def _logits(lat_ref, cb_ref):
    return LOGIT_SCALE * lax.dot_general(
        lat_ref[...], cb_ref[...], (((1,), (1,)), ((), ())), preferred_element_type=jnp.float32
    )


def _lane_groups(x):
    return [x[:, g * 128:(g + 1) * 128] for g in range(x.shape[1] // 128)]


def _stats_kernel(lat_ref, cb_ref, m_ref, s_ref, t_ref):
    j = pl.program_id(1)

    @pl.when(j == 0)
    def _():
        m_ref[...] = jnp.full(m_ref.shape, -jnp.inf, jnp.float32)
        s_ref[...] = jnp.zeros(s_ref.shape, jnp.float32)
        t_ref[...] = jnp.zeros(t_ref.shape, jnp.float32)

    groups = _lane_groups(_logits(lat_ref, cb_ref))
    m_old = m_ref[...]
    m_new = functools.reduce(jnp.maximum, groups, m_old)
    rescale = jnp.exp(m_old - m_new)
    s_acc = s_ref[...] * rescale
    t_acc = t_ref[...] * rescale
    for g in groups:
        e = jnp.exp(g - m_new)
        s_acc = s_acc + e
        t_acc = t_acc + e * g
    m_ref[...] = m_new
    s_ref[...] = s_acc
    t_ref[...] = t_acc


def row_stats(lat, cb, interpret=False):
    t_all, d = lat.shape
    s_all = cb.shape[0]
    tm, tn = min(TM, t_all), min(TN, s_all)
    row = pl.BlockSpec((tm, 128), lambda i, j: (i, 0))
    lanes = jax.ShapeDtypeStruct((t_all, 128), jnp.float32)
    return pl.pallas_call(
        _stats_kernel,
        grid=(t_all // tm, s_all // tn),
        in_specs=[
            pl.BlockSpec((tm, d), lambda i, j: (i, 0)),
            pl.BlockSpec((tn, d), lambda i, j: (j, 0)),
        ],
        out_specs=[row, row, row],
        out_shape=[lanes] * 3,
        compiler_params=pltpu.CompilerParams(
            dimension_semantics=("arbitrary", "arbitrary"), vmem_limit_bytes=VMEM
        ),
        interpret=interpret,
    )(lat, cb)


def _usage_kernel(lat_ref, cb_ref, lt_ref, out_ref):
    i = pl.program_id(1)
    probs = jnp.exp(_logits(lat_ref, cb_ref) - lt_ref[:, 0:1])
    col = jnp.sum(probs, axis=0, keepdims=True)

    @pl.when(i == 0)
    def _():
        out_ref[...] = col

    @pl.when(i > 0)
    def _():
        out_ref[...] = out_ref[...] + col


def usage_sums(lat, cb, lt, interpret=False):
    t_all, d = lat.shape
    s_all = cb.shape[0]
    tm, tn = min(TM, t_all), min(TN, s_all)
    return pl.pallas_call(
        _usage_kernel,
        grid=(s_all // tn, t_all // tm),
        in_specs=[
            pl.BlockSpec((tm, d), lambda j, i: (i, 0)),
            pl.BlockSpec((tn, d), lambda j, i: (j, 0)),
            pl.BlockSpec((tm, 128), lambda j, i: (i, 0)),
        ],
        out_specs=pl.BlockSpec((1, tn), lambda j, i: (0, j)),
        out_shape=jax.ShapeDtypeStruct((1, s_all), jnp.float32),
        compiler_params=pltpu.CompilerParams(
            dimension_semantics=("arbitrary", "arbitrary"), vmem_limit_bytes=VMEM
        ),
        interpret=interpret,
    )(lat, cb, lt)


def _spread_kernel(lat_ref, cb_ref, lt_ref, w_ref, out_ref):
    j = pl.program_id(1)
    groups = _lane_groups(jnp.exp(_logits(lat_ref, cb_ref) - lt_ref[:, 0:1]))
    weights = _lane_groups(w_ref[...])
    part = groups[0] * weights[0]
    for g, w in zip(groups[1:], weights[1:]):
        part = part + g * w

    @pl.when(j == 0)
    def _():
        out_ref[...] = part

    @pl.when(j > 0)
    def _():
        out_ref[...] = out_ref[...] + part


def spread_sums(lat, cb, lt, w, interpret=False):
    t_all, d = lat.shape
    s_all = cb.shape[0]
    tm, tn = min(TM, t_all), min(TN, s_all)
    return pl.pallas_call(
        _spread_kernel,
        grid=(t_all // tm, s_all // tn),
        in_specs=[
            pl.BlockSpec((tm, d), lambda i, j: (i, 0)),
            pl.BlockSpec((tn, d), lambda i, j: (j, 0)),
            pl.BlockSpec((tm, 128), lambda i, j: (i, 0)),
            pl.BlockSpec((1, tn), lambda i, j: (0, j)),
        ],
        out_specs=pl.BlockSpec((tm, 128), lambda i, j: (i, 0)),
        out_shape=jax.ShapeDtypeStruct((t_all, 128), jnp.float32),
        compiler_params=pltpu.CompilerParams(
            dimension_semantics=("arbitrary", "arbitrary"), vmem_limit_bytes=VMEM
        ),
        interpret=interpret,
    )(lat, cb, lt, w)


def _grad_kernel(lat_ref, cb_ref, lt_ref, rowc_ref, tgt_ref, hw_ref, *refs, tm, tn, carry):
    if carry:
        prev_ref, tok_ref, cbg_ref = refs
    else:
        tok_ref, cbg_ref = refs
    j = pl.program_id(0)
    i = pl.program_id(1)
    logits = _logits(lat_ref, cb_ref)
    probs = jnp.exp(logits - lt_ref[:, 0:1])
    cols = j * tn + lax.broadcasted_iota(jnp.int32, logits.shape, 1)
    hit = (cols == tgt_ref[:, 0:1]).astype(jnp.float32)
    grad = (probs * (rowc_ref[:, 0:1] + hw_ref[...] - 0.5 * logits) - hit).astype(jnp.bfloat16)
    tok = jnp.dot(grad, cb_ref[...], preferred_element_type=jnp.float32)
    cbg = lax.dot_general(
        grad, lat_ref[...], (((0,), (0,)), ((), ())), preferred_element_type=jnp.float32
    )
    rows = pl.ds(pl.multiple_of(i * tm, tm), tm)

    @pl.when(j == 0)
    def _():
        tok_ref[rows, :] = tok

    @pl.when(j > 0)
    def _():
        tok_ref[rows, :] = tok_ref[rows, :] + tok

    @pl.when(i == 0)
    def _():
        cbg_ref[...] = prev_ref[...] + cbg if carry else cbg

    @pl.when(i > 0)
    def _():
        cbg_ref[...] = cbg_ref[...] + cbg


def grads(lat, cb, lt, rowc, tgt, hw, prev=None, interpret=False):
    t_all, d = lat.shape
    s_all = cb.shape[0]
    tm, tn = min(TM, t_all), min(TN, s_all)
    row = pl.BlockSpec((tm, 128), lambda j, i: (i, 0))
    return pl.pallas_call(
        functools.partial(_grad_kernel, tm=tm, tn=tn, carry=prev is not None),
        grid=(s_all // tn, t_all // tm),
        in_specs=[
            pl.BlockSpec((tm, d), lambda j, i: (i, 0)),
            pl.BlockSpec((tn, d), lambda j, i: (j, 0)),
            row,
            row,
            row,
            pl.BlockSpec((1, tn), lambda j, i: (0, j)),
        ] + ([] if prev is None else [pl.BlockSpec((tn, d), lambda j, i: (j, 0))]),
        out_specs=[
            pl.BlockSpec((t_all, d), lambda j, i: (0, 0)),
            pl.BlockSpec((tn, d), lambda j, i: (j, 0)),
        ],
        out_shape=[
            jax.ShapeDtypeStruct((t_all, d), jnp.float32),
            jax.ShapeDtypeStruct((s_all, d), jnp.float32),
        ],
        compiler_params=pltpu.CompilerParams(
            dimension_semantics=("arbitrary", "arbitrary"), vmem_limit_bytes=VMEM
        ),
        input_output_aliases={} if prev is None else {6: 1},
        interpret=interpret,
    )(lat, cb, lt, rowc, tgt, hw, *([] if prev is None else [prev]))


def butterfly(values, axis, count, combine):
    step = 1
    while step < count:
        pairs = [(i, i ^ step) for i in range(count)]
        values = combine(values, lax.ppermute(values, axis, pairs))
        step *= 2
    return values


def butterfly_gather(block, axis, count):
    index = lax.axis_index(axis)
    step = 1
    while step < count:
        pairs = [(i, i ^ step) for i in range(count)]
        other = lax.ppermute(block, axis, pairs)
        low = (index // step) % 2 == 0
        block = jnp.where(low, jnp.concatenate([block, other]), jnp.concatenate([other, block]))
        step *= 2
    return block


def softmax_merge(a, b):
    top = jnp.maximum(a[0], b[0])
    wa = jnp.exp(a[0] - top)
    wb = jnp.exp(b[0] - top)
    return jnp.stack([top, a[1] * wa + b[1] * wb, a[2] * wa + b[2] * wb])


def lanes(row_values):
    return jnp.broadcast_to(row_values[:, None], (row_values.shape[0], 128))


def is_pow2(n):
    return n & (n - 1) == 0


def rotate(latent, code_vec, cotangent):
    latent_norm = jnp.sqrt(jnp.sum(latent * latent, axis=1, keepdims=True) + norm_eps)
    code_norm = jnp.sqrt(jnp.sum(code_vec * code_vec, axis=1, keepdims=True) + norm_eps)
    latent_dir = latent / latent_norm
    code_dir = code_vec / code_norm
    cosine = jnp.sum(latent_dir * code_dir, axis=1, keepdims=True)
    summed = latent_dir + code_dir
    along = jnp.sum(summed * cotangent, axis=1, keepdims=True)
    facing = jnp.sum(code_dir * cotangent, axis=1, keepdims=True)
    turned = (
        cotangent
        - summed * along / jnp.maximum(1.0 + cosine, cos_floor)
        + 2.0 * latent_dir * facing
    )
    return code_norm / latent_norm * turned


def local(latents, codebook, hard_code, upstream):
    n_dp = lax.axis_size("dp")
    n_code = lax.axis_size("code")
    n_all = n_dp * n_code
    dp_i = lax.axis_index("dp")
    code_i = lax.axis_index("code")
    row_count = latents.shape[0]
    code_count = codebook.shape[0]
    width = latents.shape[1]
    tokens_total = row_count * n_dp
    slab = code_count // n_dp
    owned = row_count // n_code
    all_lat = lax.all_gather(latents, "dp", tiled=True)
    if is_pow2(n_dp):
        all_hard = butterfly_gather(hard_code, "dp", n_dp)
    else:
        all_hard = lax.all_gather(hard_code, "dp", tiled=True)
    my_codes = lax.dynamic_slice_in_dim(codebook, dp_i * slab, slab, axis=0)
    offset = code_i * code_count + dp_i * slab

    lane_top, lane_total, lane_moment = row_stats(latents, codebook)
    shard_target = hard_code - code_i * code_count
    holder = ((shard_target >= 0) & (shard_target < code_count))[:, None]
    late_codebook, _ = lax.optimization_barrier((codebook, lane_top))
    picked_vec = jnp.where(
        holder, jnp.take(late_codebook, jnp.clip(shard_target, 0, code_count - 1), axis=0), 0
    ).astype(jnp.bfloat16)
    picked_vec = lax.all_to_all(picked_vec.reshape(n_code, owned, width), "code", 0, 0, tiled=False)
    code_vec = jnp.sum(picked_vec.astype(jnp.float32), axis=0)
    own_lat = lax.dynamic_slice_in_dim(latents, code_i * owned, owned, axis=0).astype(jnp.float32)
    own_up = lax.dynamic_slice_in_dim(upstream, code_i * owned, owned, axis=0).astype(jnp.float32)
    rotated = rotate(own_lat, code_vec, own_up)
    picked_sum = jnp.sum(LOGIT_SCALE * jnp.sum(own_lat * code_vec, axis=1))

    local_top = jnp.max(lane_top, axis=1)
    lane_scale = jnp.exp(lane_top - local_top[:, None])
    stats = jnp.stack([
        local_top, jnp.sum(lane_total * lane_scale, axis=1), jnp.sum(lane_moment * lane_scale, axis=1)
    ])
    if is_pow2(n_code):
        row_top, row_total, moment = butterfly(stats, "code", n_code, softmax_merge)
    else:
        row_top = lax.pmax(stats[0], "code")
        scale = jnp.exp(stats[0] - row_top)
        row_total, moment = lax.psum((stats[1] * scale, stats[2] * scale), "code")
    token_stats = jnp.stack([row_top + jnp.log(row_total), moment / row_total], axis=1)
    if is_pow2(n_dp):
        token_stats = butterfly_gather(token_stats, "dp", n_dp)
    else:
        token_stats = lax.all_gather(token_stats, "dp", tiled=True)
    log_total = token_stats[:, 0]
    mean_logit = token_stats[:, 1]
    entropy = log_total - mean_logit
    mean_usage = usage_sums(all_lat, my_codes, lanes(log_total))[0] / tokens_total
    log_usage = jnp.log(mean_usage + usage_eps)
    weight_term = log_usage + mean_usage / (mean_usage + usage_eps)
    spread_local = jnp.sum(spread_sums(all_lat, my_codes, lanes(log_total), weight_term[None, :]), axis=1)
    extras = jnp.stack([-jnp.sum(mean_usage * log_usage), picked_sum])
    joined = jnp.concatenate([spread_local, extras])
    if is_pow2(n_all):
        joined = butterfly(joined, BOTH, n_all, jnp.add)
    else:
        joined = lax.psum(joined, BOTH)
    spread, usage_entropy, picked_total = joined[:-2], joined[-2], joined[-1]

    row_coef = 1.0 + ENTROPY_WEIGHT * (mean_logit - spread)
    target = (all_hard - offset).astype(jnp.int32)
    chunks = 2 if owned % 2 == 0 and (tokens_total // 2) % min(TM, tokens_total // 2) == 0 else 1
    piece = owned // chunks

    def reorder(x):
        x = x.reshape((n_all, chunks, piece) + x.shape[1:])
        return jnp.swapaxes(x, 0, 1).reshape((chunks, n_all * piece) + x.shape[3:])

    lat_c, lt_c, coef_c, tgt_c = (
        reorder(v) for v in (all_lat, lanes(log_total), lanes(row_coef), lanes(target))
    )
    half_weight = ENTROPY_WEIGHT * weight_term[None, :]
    code_acc = None
    parts = []
    for q in range(chunks):
        token_acc, code_acc = grads(
            lat_c[q], my_codes, lt_c[q], coef_c[q], tgt_c[q], half_weight, prev=code_acc
        )
        token_acc = (LOGIT_SCALE * token_acc).astype(jnp.bfloat16).reshape(n_all, piece, width)
        token_acc = lax.all_to_all(token_acc, BOTH, 0, 0, tiled=False)
        parts.append(jnp.sum(token_acc.astype(jnp.float32), axis=0))
    token_sum = jnp.concatenate(parts, axis=0)
    codebook_grad = LOGIT_SCALE * code_acc
    token_grad = token_sum + rotated
    loss_terms = jnp.stack([
        (jnp.sum(log_total) - picked_total) / tokens_total,
        jnp.sum(entropy) / tokens_total,
        usage_entropy,
    ])
    return (token_grad, codebook_grad, loss_terms)


def solution(mesh):
    placed = (P("dp", None), P("code", None), P("dp"), P("dp", None))
    return jax.shard_map(
        local,
        mesh=mesh,
        in_specs=placed,
        out_specs=(P(("dp", "code"), None), P(("code", "dp"), None), P()),
        check_vma=False,
    )
```

```python
import jax
import jax.numpy as jnp
from jax import lax
from jax.experimental import pallas as pl
from jax.experimental.pallas import tpu as pltpu
from jax.sharding import PartitionSpec as P
import functools

LOGIT_SCALE = 5.0
ENTROPY_WEIGHT = 0.5
usage_eps = 1e-06
norm_eps = 1e-06
cos_floor = 0.25
BOTH = ("dp", "code")
TM = 512
TN = 4096
VMEM = 48 * 1024 * 1024


def _logits(lat_ref, cb_ref):
    return LOGIT_SCALE * lax.dot_general(
        lat_ref[...], cb_ref[...], (((1,), (1,)), ((), ())), preferred_element_type=jnp.float32
    )


def _lane_groups(x):
    return [x[:, g * 128:(g + 1) * 128] for g in range(x.shape[1] // 128)]


def _stats_kernel(lat_ref, cb_ref, m_ref, s_ref, t_ref):
    j = pl.program_id(1)

    @pl.when(j == 0)
    def _():
        m_ref[...] = jnp.full(m_ref.shape, -jnp.inf, jnp.float32)
        s_ref[...] = jnp.zeros(s_ref.shape, jnp.float32)
        t_ref[...] = jnp.zeros(t_ref.shape, jnp.float32)

    groups = _lane_groups(_logits(lat_ref, cb_ref))
    m_old = m_ref[...]
    m_new = functools.reduce(jnp.maximum, groups, m_old)
    rescale = jnp.exp(m_old - m_new)
    s_acc = s_ref[...] * rescale
    t_acc = t_ref[...] * rescale
    for g in groups:
        e = jnp.exp(g - m_new)
        s_acc = s_acc + e
        t_acc = t_acc + e * g
    m_ref[...] = m_new
    s_ref[...] = s_acc
    t_ref[...] = t_acc


def row_stats(lat, cb, interpret=False):
    t_all, d = lat.shape
    s_all = cb.shape[0]
    tm, tn = min(TM, t_all), min(TN, s_all)
    row = pl.BlockSpec((tm, 128), lambda i, j: (i, 0))
    lanes = jax.ShapeDtypeStruct((t_all, 128), jnp.float32)
    return pl.pallas_call(
        _stats_kernel,
        grid=(t_all // tm, s_all // tn),
        in_specs=[
            pl.BlockSpec((tm, d), lambda i, j: (i, 0)),
            pl.BlockSpec((tn, d), lambda i, j: (j, 0)),
        ],
        out_specs=[row, row, row],
        out_shape=[lanes] * 3,
        compiler_params=pltpu.CompilerParams(
            dimension_semantics=("arbitrary", "arbitrary"), vmem_limit_bytes=VMEM
        ),
        interpret=interpret,
    )(lat, cb)


def _usage_kernel(first_ref, lat_ref, cb_ref, lt_ref, out_ref):
    i = pl.program_id(1)
    probs = jnp.exp(_logits(lat_ref, cb_ref) - lt_ref[:, 0:1])
    col = jnp.sum(probs, axis=0, keepdims=True)

    @pl.when(i == 0)
    def _():
        out_ref[...] = col

    @pl.when(i > 0)
    def _():
        out_ref[...] = out_ref[...] + col


def usage_sums(lat, cb, lt, first, s_all, interpret=False):
    t_all, d = lat.shape
    tm, tn = min(TM, t_all), min(TN, s_all)
    return pl.pallas_call(
        _usage_kernel,
        grid_spec=pltpu.PrefetchScalarGridSpec(
            num_scalar_prefetch=1,
            grid=(s_all // tn, t_all // tm),
            in_specs=[
                pl.BlockSpec((tm, d), lambda j, i, f: (i, 0)),
                pl.BlockSpec((tn, d), lambda j, i, f: (j + f[0], 0)),
                pl.BlockSpec((tm, 128), lambda j, i, f: (i, 0)),
            ],
            out_specs=pl.BlockSpec((1, tn), lambda j, i, f: (0, j)),
        ),
        out_shape=jax.ShapeDtypeStruct((1, s_all), jnp.float32),
        compiler_params=pltpu.CompilerParams(
            dimension_semantics=("arbitrary", "arbitrary"), vmem_limit_bytes=VMEM
        ),
        interpret=interpret,
    )(first, lat, cb, lt)


def _spread_kernel(first_ref, lat_ref, cb_ref, lt_ref, w_ref, out_ref):
    j = pl.program_id(1)
    groups = _lane_groups(jnp.exp(_logits(lat_ref, cb_ref) - lt_ref[:, 0:1]))
    weights = _lane_groups(w_ref[...])
    part = groups[0] * weights[0]
    for g, w in zip(groups[1:], weights[1:]):
        part = part + g * w

    @pl.when(j == 0)
    def _():
        out_ref[...] = part

    @pl.when(j > 0)
    def _():
        out_ref[...] = out_ref[...] + part


def spread_sums(lat, cb, lt, w, first, s_all, interpret=False):
    t_all, d = lat.shape
    tm, tn = min(TM, t_all), min(TN, s_all)
    return pl.pallas_call(
        _spread_kernel,
        grid_spec=pltpu.PrefetchScalarGridSpec(
            num_scalar_prefetch=1,
            grid=(t_all // tm, s_all // tn),
            in_specs=[
                pl.BlockSpec((tm, d), lambda i, j, f: (i, 0)),
                pl.BlockSpec((tn, d), lambda i, j, f: (j + f[0], 0)),
                pl.BlockSpec((tm, 128), lambda i, j, f: (i, 0)),
                pl.BlockSpec((1, tn), lambda i, j, f: (0, j)),
            ],
            out_specs=pl.BlockSpec((tm, 128), lambda i, j, f: (i, 0)),
        ),
        out_shape=jax.ShapeDtypeStruct((t_all, 128), jnp.float32),
        compiler_params=pltpu.CompilerParams(
            dimension_semantics=("arbitrary", "arbitrary"), vmem_limit_bytes=VMEM
        ),
        interpret=interpret,
    )(first, lat, cb, lt, w)


def _grad_kernel(first_ref, lat_ref, cb_ref, lt_ref, rowc_ref, tgt_ref, hw_ref, *refs, tm, tn, carry):
    if carry:
        prev_ref, tok_ref, cbg_ref = refs
    else:
        tok_ref, cbg_ref = refs
    j = pl.program_id(0)
    i = pl.program_id(1)
    logits = _logits(lat_ref, cb_ref)
    probs = jnp.exp(logits - lt_ref[:, 0:1])
    cols = j * tn + lax.broadcasted_iota(jnp.int32, logits.shape, 1)
    hit = (cols == tgt_ref[:, 0:1]).astype(jnp.float32)
    grad = (probs * (rowc_ref[:, 0:1] + hw_ref[...] - 0.5 * logits) - hit).astype(jnp.bfloat16)
    tok = jnp.dot(grad, cb_ref[...], preferred_element_type=jnp.float32)
    cbg = lax.dot_general(
        grad, lat_ref[...], (((0,), (0,)), ((), ())), preferred_element_type=jnp.float32
    )
    rows = pl.ds(pl.multiple_of(i * tm, tm), tm)

    @pl.when(j == 0)
    def _():
        tok_ref[rows, :] = tok

    @pl.when(j > 0)
    def _():
        tok_ref[rows, :] = tok_ref[rows, :] + tok

    @pl.when(i == 0)
    def _():
        cbg_ref[...] = prev_ref[...] + cbg if carry else cbg

    @pl.when(i > 0)
    def _():
        cbg_ref[...] = cbg_ref[...] + cbg


def grads(lat, cb, lt, rowc, tgt, hw, first, s_all, prev=None, interpret=False):
    t_all, d = lat.shape
    tm, tn = min(TM, t_all), min(TN, s_all)
    row = pl.BlockSpec((tm, 128), lambda j, i, f: (i, 0))
    slab_block = pl.BlockSpec((tn, d), lambda j, i, f: (j, 0))
    return pl.pallas_call(
        functools.partial(_grad_kernel, tm=tm, tn=tn, carry=prev is not None),
        grid_spec=pltpu.PrefetchScalarGridSpec(
            num_scalar_prefetch=1,
            grid=(s_all // tn, t_all // tm),
            in_specs=[
                pl.BlockSpec((tm, d), lambda j, i, f: (i, 0)),
                pl.BlockSpec((tn, d), lambda j, i, f: (j + f[0], 0)),
                row,
                row,
                row,
                pl.BlockSpec((1, tn), lambda j, i, f: (0, j)),
            ] + ([] if prev is None else [slab_block]),
            out_specs=[pl.BlockSpec((t_all, d), lambda j, i, f: (0, 0)), slab_block],
        ),
        out_shape=[
            jax.ShapeDtypeStruct((t_all, d), jnp.float32),
            jax.ShapeDtypeStruct((s_all, d), jnp.float32),
        ],
        compiler_params=pltpu.CompilerParams(
            dimension_semantics=("arbitrary", "arbitrary"), vmem_limit_bytes=VMEM
        ),
        input_output_aliases={} if prev is None else {7: 1},
        interpret=interpret,
    )(first, lat, cb, lt, rowc, tgt, hw, *([] if prev is None else [prev]))


def butterfly(values, axis, count, combine):
    step = 1
    while step < count:
        pairs = [(i, i ^ step) for i in range(count)]
        values = combine(values, lax.ppermute(values, axis, pairs))
        step *= 2
    return values


def butterfly_gather(block, axis, count):
    index = lax.axis_index(axis)
    step = 1
    while step < count:
        pairs = [(i, i ^ step) for i in range(count)]
        other = lax.ppermute(block, axis, pairs)
        low = (index // step) % 2 == 0
        block = jnp.where(low, jnp.concatenate([block, other]), jnp.concatenate([other, block]))
        step *= 2
    return block


def softmax_merge(a, b):
    top = jnp.maximum(a[0], b[0])
    wa = jnp.exp(a[0] - top)
    wb = jnp.exp(b[0] - top)
    return jnp.stack([top, a[1] * wa + b[1] * wb, a[2] * wa + b[2] * wb])


def lanes(row_values):
    return jnp.broadcast_to(row_values[:, None], (row_values.shape[0], 128))


def is_pow2(n):
    return n & (n - 1) == 0


def rotate(latent, code_vec, cotangent):
    latent_norm = jnp.sqrt(jnp.sum(latent * latent, axis=1, keepdims=True) + norm_eps)
    code_norm = jnp.sqrt(jnp.sum(code_vec * code_vec, axis=1, keepdims=True) + norm_eps)
    latent_dir = latent / latent_norm
    code_dir = code_vec / code_norm
    cosine = jnp.sum(latent_dir * code_dir, axis=1, keepdims=True)
    summed = latent_dir + code_dir
    along = jnp.sum(summed * cotangent, axis=1, keepdims=True)
    facing = jnp.sum(code_dir * cotangent, axis=1, keepdims=True)
    turned = (
        cotangent
        - summed * along / jnp.maximum(1.0 + cosine, cos_floor)
        + 2.0 * latent_dir * facing
    )
    return code_norm / latent_norm * turned


def local(latents, codebook, hard_code, upstream):
    n_dp = lax.axis_size("dp")
    n_code = lax.axis_size("code")
    n_all = n_dp * n_code
    dp_i = lax.axis_index("dp")
    code_i = lax.axis_index("code")
    row_count = latents.shape[0]
    code_count = codebook.shape[0]
    width = latents.shape[1]
    tokens_total = row_count * n_dp
    slab = code_count // n_dp
    owned = row_count // n_code
    all_lat = lax.all_gather(latents, "dp", tiled=True)
    if is_pow2(n_dp):
        all_hard = butterfly_gather(hard_code, "dp", n_dp)
    else:
        all_hard = lax.all_gather(hard_code, "dp", tiled=True)
    first = jnp.reshape(dp_i * (slab // min(TN, slab)), (1,)).astype(jnp.int32)
    offset = code_i * code_count + dp_i * slab

    lane_top, lane_total, lane_moment = row_stats(latents, codebook)
    shard_target = hard_code - code_i * code_count
    holder = ((shard_target >= 0) & (shard_target < code_count))[:, None]
    late_codebook, _ = lax.optimization_barrier((codebook, lane_top))
    picked_vec = jnp.where(
        holder, jnp.take(late_codebook, jnp.clip(shard_target, 0, code_count - 1), axis=0), 0
    ).astype(jnp.bfloat16)
    picked_vec = lax.all_to_all(picked_vec.reshape(n_code, owned, width), "code", 0, 0, tiled=False)
    code_vec = jnp.sum(picked_vec.astype(jnp.float32), axis=0)
    own_lat = lax.dynamic_slice_in_dim(latents, code_i * owned, owned, axis=0).astype(jnp.float32)
    own_up = lax.dynamic_slice_in_dim(upstream, code_i * owned, owned, axis=0).astype(jnp.float32)
    rotated = rotate(own_lat, code_vec, own_up)
    picked_sum = jnp.sum(LOGIT_SCALE * jnp.sum(own_lat * code_vec, axis=1))

    local_top = jnp.max(lane_top, axis=1)
    lane_scale = jnp.exp(lane_top - local_top[:, None])
    stats = jnp.stack([
        local_top, jnp.sum(lane_total * lane_scale, axis=1), jnp.sum(lane_moment * lane_scale, axis=1)
    ])
    if is_pow2(n_code):
        row_top, row_total, moment = butterfly(stats, "code", n_code, softmax_merge)
    else:
        row_top = lax.pmax(stats[0], "code")
        scale = jnp.exp(stats[0] - row_top)
        row_total, moment = lax.psum((stats[1] * scale, stats[2] * scale), "code")
    token_stats = jnp.stack([row_top + jnp.log(row_total), moment / row_total], axis=1)
    if is_pow2(n_dp):
        token_stats = butterfly_gather(token_stats, "dp", n_dp)
    else:
        token_stats = lax.all_gather(token_stats, "dp", tiled=True)
    log_total = token_stats[:, 0]
    mean_logit = token_stats[:, 1]
    entropy = log_total - mean_logit
    mean_usage = usage_sums(all_lat, codebook, lanes(log_total), first, slab)[0] / tokens_total
    log_usage = jnp.log(mean_usage + usage_eps)
    weight_term = log_usage + mean_usage / (mean_usage + usage_eps)
    spread_local = jnp.sum(spread_sums(all_lat, codebook, lanes(log_total), weight_term[None, :], first, slab), axis=1)
    extras = jnp.stack([-jnp.sum(mean_usage * log_usage), picked_sum])
    joined = jnp.concatenate([spread_local, extras])
    if is_pow2(n_all):
        joined = butterfly(joined, BOTH, n_all, jnp.add)
    else:
        joined = lax.psum(joined, BOTH)
    spread, usage_entropy, picked_total = joined[:-2], joined[-2], joined[-1]

    row_coef = 1.0 + ENTROPY_WEIGHT * (mean_logit - spread)
    target = (all_hard - offset).astype(jnp.int32)
    chunks = 2 if owned % 2 == 0 and (tokens_total // 2) % min(TM, tokens_total // 2) == 0 else 1
    piece = owned // chunks

    def reorder(x):
        x = x.reshape((n_all, chunks, piece) + x.shape[1:])
        return jnp.swapaxes(x, 0, 1).reshape((chunks, n_all * piece) + x.shape[3:])

    lat_c, lt_c, coef_c, tgt_c = (
        reorder(v) for v in (all_lat, lanes(log_total), lanes(row_coef), lanes(target))
    )
    half_weight = ENTROPY_WEIGHT * weight_term[None, :]
    code_acc = None
    parts = []
    for q in range(chunks):
        token_acc, code_acc = grads(
            lat_c[q], codebook, lt_c[q], coef_c[q], tgt_c[q], half_weight, first, slab, prev=code_acc
        )
        token_acc = (LOGIT_SCALE * token_acc).astype(jnp.bfloat16).reshape(n_all, piece, width)
        token_acc = lax.all_to_all(token_acc, BOTH, 0, 0, tiled=False)
        parts.append(jnp.sum(token_acc.astype(jnp.float32), axis=0))
    token_sum = jnp.concatenate(parts, axis=0)
    codebook_grad = LOGIT_SCALE * code_acc
    token_grad = token_sum + rotated
    loss_terms = jnp.stack([
        (jnp.sum(log_total) - picked_total) / tokens_total,
        jnp.sum(entropy) / tokens_total,
        usage_entropy,
    ])
    return (token_grad, codebook_grad, loss_terms)


def solution(mesh):
    placed = (P("dp", None), P("code", None), P("dp"), P("dp", None))
    return jax.shard_map(
        local,
        mesh=mesh,
        in_specs=placed,
        out_specs=(P(("dp", "code"), None), P(("code", "dp"), None), P()),
        check_vma=False,
    )
```

```python
import jax
import jax.numpy as jnp
from jax import lax
from jax.experimental import pallas as pl
from jax.experimental.pallas import tpu as pltpu
from jax.sharding import PartitionSpec as P
import functools

LOGIT_SCALE = 5.0
ENTROPY_WEIGHT = 0.5
usage_eps = 1e-06
norm_eps = 1e-06
cos_floor = 0.25
BOTH = ("dp", "code")
TM = 512
TN = 4096
VMEM = 48 * 1024 * 1024


def _logits(lat_ref, cb_ref):
    return LOGIT_SCALE * lax.dot_general(
        lat_ref[...], cb_ref[...], (((1,), (1,)), ((), ())), preferred_element_type=jnp.float32
    )


def _lane_groups(x):
    return [x[:, g * 128:(g + 1) * 128] for g in range(x.shape[1] // 128)]


def _stats_kernel(lat_ref, cb_ref, m_ref, s_ref, t_ref):
    j = pl.program_id(1)

    @pl.when(j == 0)
    def _():
        m_ref[...] = jnp.full(m_ref.shape, -jnp.inf, jnp.float32)
        s_ref[...] = jnp.zeros(s_ref.shape, jnp.float32)
        t_ref[...] = jnp.zeros(t_ref.shape, jnp.float32)

    groups = _lane_groups(_logits(lat_ref, cb_ref))
    m_old = m_ref[...]
    m_new = functools.reduce(jnp.maximum, groups, m_old)
    rescale = jnp.exp(m_old - m_new)
    s_acc = s_ref[...] * rescale
    t_acc = t_ref[...] * rescale
    for g in groups:
        e = jnp.exp(g - m_new)
        s_acc = s_acc + e
        t_acc = t_acc + e * g
    m_ref[...] = m_new
    s_ref[...] = s_acc
    t_ref[...] = t_acc


def row_stats(lat, cb, interpret=False):
    t_all, d = lat.shape
    s_all = cb.shape[0]
    tm, tn = min(TM, t_all), min(TN, s_all)
    row = pl.BlockSpec((tm, 128), lambda i, j: (i, 0))
    lanes = jax.ShapeDtypeStruct((t_all, 128), jnp.float32)
    return pl.pallas_call(
        _stats_kernel,
        grid=(t_all // tm, s_all // tn),
        in_specs=[
            pl.BlockSpec((tm, d), lambda i, j: (i, 0)),
            pl.BlockSpec((tn, d), lambda i, j: (j, 0)),
        ],
        out_specs=[row, row, row],
        out_shape=[lanes] * 3,
        compiler_params=pltpu.CompilerParams(
            dimension_semantics=("arbitrary", "arbitrary"), vmem_limit_bytes=VMEM
        ),
        interpret=interpret,
    )(lat, cb)


def _usage_kernel(first_ref, lat_ref, cb_ref, lt_ref, out_ref):
    i = pl.program_id(1)
    probs = jnp.exp(_logits(lat_ref, cb_ref) - lt_ref[:, 0:1])
    col = jnp.sum(probs, axis=0, keepdims=True)

    @pl.when(i == 0)
    def _():
        out_ref[...] = col

    @pl.when(i > 0)
    def _():
        out_ref[...] = out_ref[...] + col


def usage_sums(lat, cb, lt, first, s_all, interpret=False):
    t_all, d = lat.shape
    tm, tn = min(TM, t_all), min(TN, s_all)
    return pl.pallas_call(
        _usage_kernel,
        grid_spec=pltpu.PrefetchScalarGridSpec(
            num_scalar_prefetch=1,
            grid=(s_all // tn, t_all // tm),
            in_specs=[
                pl.BlockSpec((tm, d), lambda j, i, f: (i, 0)),
                pl.BlockSpec((tn, d), lambda j, i, f: (j + f[0], 0)),
                pl.BlockSpec((tm, 128), lambda j, i, f: (i, 0)),
            ],
            out_specs=pl.BlockSpec((1, tn), lambda j, i, f: (0, j)),
        ),
        out_shape=jax.ShapeDtypeStruct((1, s_all), jnp.float32),
        compiler_params=pltpu.CompilerParams(
            dimension_semantics=("arbitrary", "arbitrary"), vmem_limit_bytes=VMEM
        ),
        interpret=interpret,
    )(first, lat, cb, lt)


def _spread_kernel(first_ref, lat_ref, cb_ref, lt_ref, w_ref, out_ref):
    j = pl.program_id(1)
    groups = _lane_groups(jnp.exp(_logits(lat_ref, cb_ref) - lt_ref[:, 0:1]))
    weights = _lane_groups(w_ref[...])
    part = groups[0] * weights[0]
    for g, w in zip(groups[1:], weights[1:]):
        part = part + g * w

    @pl.when(j == 0)
    def _():
        out_ref[...] = part

    @pl.when(j > 0)
    def _():
        out_ref[...] = out_ref[...] + part


def spread_sums(lat, cb, lt, w, first, s_all, interpret=False):
    t_all, d = lat.shape
    tm, tn = min(TM, t_all), min(TN, s_all)
    return pl.pallas_call(
        _spread_kernel,
        grid_spec=pltpu.PrefetchScalarGridSpec(
            num_scalar_prefetch=1,
            grid=(t_all // tm, s_all // tn),
            in_specs=[
                pl.BlockSpec((tm, d), lambda i, j, f: (i, 0)),
                pl.BlockSpec((tn, d), lambda i, j, f: (j + f[0], 0)),
                pl.BlockSpec((tm, 128), lambda i, j, f: (i, 0)),
                pl.BlockSpec((1, tn), lambda i, j, f: (0, j)),
            ],
            out_specs=pl.BlockSpec((tm, 128), lambda i, j, f: (i, 0)),
        ),
        out_shape=jax.ShapeDtypeStruct((t_all, 128), jnp.float32),
        compiler_params=pltpu.CompilerParams(
            dimension_semantics=("arbitrary", "arbitrary"), vmem_limit_bytes=VMEM
        ),
        interpret=interpret,
    )(first, lat, cb, lt, w)


def _grad_kernel(first_ref, lat_ref, cb_ref, lt_ref, rowc_ref, tgt_ref, hw_ref, *refs, tm, tn, carry):
    if carry:
        prev_ref, tok_ref, cbg_ref = refs
    else:
        tok_ref, cbg_ref = refs
    j = pl.program_id(0)
    i = pl.program_id(1)
    logits = _logits(lat_ref, cb_ref)
    probs = jnp.exp(logits - lt_ref[:, 0:1])
    cols = j * tn + lax.broadcasted_iota(jnp.int32, logits.shape, 1)
    hit = (cols == tgt_ref[:, 0:1]).astype(jnp.float32)
    grad = (probs * (rowc_ref[:, 0:1] + hw_ref[...] - 0.5 * logits) - hit).astype(jnp.bfloat16)
    tok = jnp.dot(grad, cb_ref[...], preferred_element_type=jnp.float32)
    cbg = lax.dot_general(
        grad, lat_ref[...], (((0,), (0,)), ((), ())), preferred_element_type=jnp.float32
    )
    rows = pl.ds(pl.multiple_of(i * tm, tm), tm)

    @pl.when(j == 0)
    def _():
        tok_ref[rows, :] = tok

    @pl.when(j > 0)
    def _():
        tok_ref[rows, :] = tok_ref[rows, :] + tok

    @pl.when(i == 0)
    def _():
        cbg_ref[...] = prev_ref[...] + cbg if carry else cbg

    @pl.when(i > 0)
    def _():
        cbg_ref[...] = cbg_ref[...] + cbg


def grads(lat, cb, lt, rowc, tgt, hw, first, s_all, prev=None, interpret=False):
    t_all, d = lat.shape
    tm, tn = min(TM, t_all), min(TN, s_all)
    row = pl.BlockSpec((tm, 128), lambda j, i, f: (i, 0))
    slab_block = pl.BlockSpec((tn, d), lambda j, i, f: (j, 0))
    return pl.pallas_call(
        functools.partial(_grad_kernel, tm=tm, tn=tn, carry=prev is not None),
        grid_spec=pltpu.PrefetchScalarGridSpec(
            num_scalar_prefetch=1,
            grid=(s_all // tn, t_all // tm),
            in_specs=[
                pl.BlockSpec((tm, d), lambda j, i, f: (i, 0)),
                pl.BlockSpec((tn, d), lambda j, i, f: (j + f[0], 0)),
                row,
                row,
                row,
                pl.BlockSpec((1, tn), lambda j, i, f: (0, j)),
            ] + ([] if prev is None else [slab_block]),
            out_specs=[pl.BlockSpec((t_all, d), lambda j, i, f: (0, 0)), slab_block],
        ),
        out_shape=[
            jax.ShapeDtypeStruct((t_all, d), jnp.float32),
            jax.ShapeDtypeStruct((s_all, d), jnp.float32),
        ],
        compiler_params=pltpu.CompilerParams(
            dimension_semantics=("arbitrary", "arbitrary"), vmem_limit_bytes=VMEM
        ),
        input_output_aliases={} if prev is None else {7: 1},
        interpret=interpret,
    )(first, lat, cb, lt, rowc, tgt, hw, *([] if prev is None else [prev]))


def butterfly(values, axis, count, combine):
    step = 1
    while step < count:
        pairs = [(i, i ^ step) for i in range(count)]
        values = combine(values, lax.ppermute(values, axis, pairs))
        step *= 2
    return values


def butterfly_gather(block, axis, count, dim=0):
    index = lax.axis_index(axis)
    step = 1
    while step < count:
        pairs = [(i, i ^ step) for i in range(count)]
        other = lax.ppermute(block, axis, pairs)
        low = (index // step) % 2 == 0
        block = jnp.where(
            low, jnp.concatenate([block, other], dim), jnp.concatenate([other, block], dim)
        )
        step *= 2
    return block


def softmax_merge(a, b):
    top = jnp.maximum(a[0], b[0])
    wa = jnp.exp(a[0] - top)
    wb = jnp.exp(b[0] - top)
    return jnp.stack([top, a[1] * wa + b[1] * wb, a[2] * wa + b[2] * wb])


def lanes(row_values):
    return jnp.broadcast_to(row_values[:, None], (row_values.shape[0], 128))


def is_pow2(n):
    return n & (n - 1) == 0


def rotate(latent, code_vec, cotangent):
    latent_norm = jnp.sqrt(jnp.sum(latent * latent, axis=1, keepdims=True) + norm_eps)
    code_norm = jnp.sqrt(jnp.sum(code_vec * code_vec, axis=1, keepdims=True) + norm_eps)
    latent_dir = latent / latent_norm
    code_dir = code_vec / code_norm
    cosine = jnp.sum(latent_dir * code_dir, axis=1, keepdims=True)
    summed = latent_dir + code_dir
    along = jnp.sum(summed * cotangent, axis=1, keepdims=True)
    facing = jnp.sum(code_dir * cotangent, axis=1, keepdims=True)
    turned = (
        cotangent
        - summed * along / jnp.maximum(1.0 + cosine, cos_floor)
        + 2.0 * latent_dir * facing
    )
    return code_norm / latent_norm * turned


def local(latents, codebook, hard_code, upstream):
    n_dp = lax.axis_size("dp")
    n_code = lax.axis_size("code")
    n_all = n_dp * n_code
    dp_i = lax.axis_index("dp")
    code_i = lax.axis_index("code")
    row_count = latents.shape[0]
    code_count = codebook.shape[0]
    width = latents.shape[1]
    tokens_total = row_count * n_dp
    slab = code_count // n_dp
    owned = row_count // n_code
    all_lat = lax.all_gather(latents, "dp", tiled=True)
    if is_pow2(n_dp):
        all_hard = butterfly_gather(hard_code, "dp", n_dp)
    else:
        all_hard = lax.all_gather(hard_code, "dp", tiled=True)
    first = jnp.reshape(dp_i * (slab // min(TN, slab)), (1,)).astype(jnp.int32)
    offset = code_i * code_count + dp_i * slab

    lane_top, lane_total, lane_moment = row_stats(latents, codebook)
    shard_target = hard_code - code_i * code_count
    holder = ((shard_target >= 0) & (shard_target < code_count))[:, None]
    late_codebook, _ = lax.optimization_barrier((codebook, lane_top))
    picked_vec = jnp.where(
        holder, jnp.take(late_codebook, jnp.clip(shard_target, 0, code_count - 1), axis=0), 0
    ).astype(jnp.bfloat16)
    picked_vec = lax.all_to_all(picked_vec.reshape(n_code, owned, width), "code", 0, 0, tiled=False)
    code_vec = jnp.sum(picked_vec.astype(jnp.float32), axis=0)
    own_lat = lax.dynamic_slice_in_dim(latents, code_i * owned, owned, axis=0).astype(jnp.float32)
    own_up = lax.dynamic_slice_in_dim(upstream, code_i * owned, owned, axis=0).astype(jnp.float32)
    rotated = rotate(own_lat, code_vec, own_up)
    picked_sum = jnp.sum(LOGIT_SCALE * jnp.sum(own_lat * code_vec, axis=1))

    local_top = jnp.max(lane_top, axis=1)
    lane_scale = jnp.exp(lane_top - local_top[:, None])
    stats = jnp.stack([
        local_top, jnp.sum(lane_total * lane_scale, axis=1), jnp.sum(lane_moment * lane_scale, axis=1)
    ])
    if is_pow2(n_code):
        row_top, row_total, moment = butterfly(stats, "code", n_code, softmax_merge)
    else:
        row_top = lax.pmax(stats[0], "code")
        scale = jnp.exp(stats[0] - row_top)
        row_total, moment = lax.psum((stats[1] * scale, stats[2] * scale), "code")
    token_stats = jnp.stack([row_top + jnp.log(row_total), moment / row_total])
    if is_pow2(n_dp):
        token_stats = butterfly_gather(token_stats, "dp", n_dp, dim=1)
    else:
        token_stats = lax.all_gather(token_stats, "dp", axis=1, tiled=True)
    log_total = token_stats[0]
    mean_logit = token_stats[1]
    entropy = log_total - mean_logit
    mean_usage = usage_sums(all_lat, codebook, lanes(log_total), first, slab)[0] / tokens_total
    log_usage = jnp.log(mean_usage + usage_eps)
    weight_term = log_usage + mean_usage / (mean_usage + usage_eps)
    spread_local = jnp.sum(spread_sums(all_lat, codebook, lanes(log_total), weight_term[None, :], first, slab), axis=1)
    extras = jnp.stack([-jnp.sum(mean_usage * log_usage), picked_sum])
    joined = jnp.concatenate([spread_local, extras])
    if is_pow2(n_all):
        joined = butterfly(joined, BOTH, n_all, jnp.add)
    else:
        joined = lax.psum(joined, BOTH)
    spread, usage_entropy, picked_total = joined[:-2], joined[-2], joined[-1]

    row_coef = 1.0 + ENTROPY_WEIGHT * (mean_logit - spread)
    target = (all_hard - offset).astype(jnp.int32)
    chunks = 2 if owned % 2 == 0 and (tokens_total // 2) % min(TM, tokens_total // 2) == 0 else 1
    piece = owned // chunks

    def reorder(x):
        x = x.reshape((n_all, chunks, piece) + x.shape[1:])
        return jnp.swapaxes(x, 0, 1).reshape((chunks, n_all * piece) + x.shape[3:])

    lat_c, lt_c, coef_c, tgt_c = (
        reorder(v) for v in (all_lat, lanes(log_total), lanes(row_coef), lanes(target))
    )
    half_weight = ENTROPY_WEIGHT * weight_term[None, :]
    code_acc = None
    parts = []
    for q in range(chunks):
        token_acc, code_acc = grads(
            lat_c[q], codebook, lt_c[q], coef_c[q], tgt_c[q], half_weight, first, slab, prev=code_acc
        )
        token_acc = (LOGIT_SCALE * token_acc).astype(jnp.bfloat16).reshape(n_all, piece, width)
        token_acc = lax.all_to_all(token_acc, BOTH, 0, 0, tiled=False)
        parts.append(jnp.sum(token_acc.astype(jnp.float32), axis=0))
    token_sum = jnp.concatenate(parts, axis=0)
    codebook_grad = LOGIT_SCALE * code_acc
    token_grad = token_sum + rotated
    loss_terms = jnp.stack([
        (jnp.sum(log_total) - picked_total) / tokens_total,
        jnp.sum(entropy) / tokens_total,
        usage_entropy,
    ])
    return (token_grad, codebook_grad, loss_terms)


def solution(mesh):
    placed = (P("dp", None), P("code", None), P("dp"), P("dp", None))
    return jax.shard_map(
        local,
        mesh=mesh,
        in_specs=placed,
        out_specs=(P(("dp", "code"), None), P(("code", "dp"), None), P()),
        check_vma=False,
    )
```

```python
import jax
import jax.numpy as jnp
from jax import lax
from jax.experimental import pallas as pl
from jax.experimental.pallas import tpu as pltpu
from jax.sharding import PartitionSpec as P
import functools

LOGIT_SCALE = 5.0
ENTROPY_WEIGHT = 0.5
usage_eps = 1e-06
norm_eps = 1e-06
cos_floor = 0.25
BOTH = ("dp", "code")
TM = 512
TN = 4096
VMEM = 48 * 1024 * 1024


def _logits(lat_ref, cb_ref):
    return LOGIT_SCALE * lax.dot_general(
        lat_ref[...], cb_ref[...], (((1,), (1,)), ((), ())), preferred_element_type=jnp.float32
    )


def _lane_groups(x):
    return [x[:, g * 128:(g + 1) * 128] for g in range(x.shape[1] // 128)]


def _stats_kernel(lat_ref, cb_ref, m_ref, s_ref, t_ref):
    j = pl.program_id(1)

    @pl.when(j == 0)
    def _():
        m_ref[...] = jnp.full(m_ref.shape, -jnp.inf, jnp.float32)
        s_ref[...] = jnp.zeros(s_ref.shape, jnp.float32)
        t_ref[...] = jnp.zeros(t_ref.shape, jnp.float32)

    groups = _lane_groups(_logits(lat_ref, cb_ref))
    m_old = m_ref[...]
    m_new = functools.reduce(jnp.maximum, groups, m_old)
    rescale = jnp.exp(m_old - m_new)
    s_acc = s_ref[...] * rescale
    t_acc = t_ref[...] * rescale
    for g in groups:
        e = jnp.exp(g - m_new)
        s_acc = s_acc + e
        t_acc = t_acc + e * g
    m_ref[...] = m_new
    s_ref[...] = s_acc
    t_ref[...] = t_acc


def row_stats(lat, cb, interpret=False):
    t_all, d = lat.shape
    s_all = cb.shape[0]
    tm, tn = min(TM, t_all), min(TN, s_all)
    row = pl.BlockSpec((tm, 128), lambda i, j: (i, 0))
    lanes = jax.ShapeDtypeStruct((t_all, 128), jnp.float32)
    return pl.pallas_call(
        _stats_kernel,
        grid=(t_all // tm, s_all // tn),
        in_specs=[
            pl.BlockSpec((tm, d), lambda i, j: (i, 0)),
            pl.BlockSpec((tn, d), lambda i, j: (j, 0)),
        ],
        out_specs=[row, row, row],
        out_shape=[lanes] * 3,
        compiler_params=pltpu.CompilerParams(
            dimension_semantics=("arbitrary", "arbitrary"), vmem_limit_bytes=VMEM
        ),
        interpret=interpret,
    )(lat, cb)


def _usage_kernel(first_ref, lat_ref, cb_ref, lt_ref, out_ref):
    i = pl.program_id(1)
    probs = jnp.exp(_logits(lat_ref, cb_ref) - lt_ref[:, 0:1])
    col = jnp.sum(probs, axis=0, keepdims=True)

    @pl.when(i == 0)
    def _():
        out_ref[...] = col

    @pl.when(i > 0)
    def _():
        out_ref[...] = out_ref[...] + col


def usage_sums(lat, cb, lt, first, s_all, interpret=False):
    t_all, d = lat.shape
    tm, tn = min(TM, t_all), min(TN, s_all)
    return pl.pallas_call(
        _usage_kernel,
        grid_spec=pltpu.PrefetchScalarGridSpec(
            num_scalar_prefetch=1,
            grid=(s_all // tn, t_all // tm),
            in_specs=[
                pl.BlockSpec((tm, d), lambda j, i, f: (i, 0)),
                pl.BlockSpec((tn, d), lambda j, i, f: (j + f[0], 0)),
                pl.BlockSpec((tm, 128), lambda j, i, f: (i, 0)),
            ],
            out_specs=pl.BlockSpec((1, tn), lambda j, i, f: (0, j)),
        ),
        out_shape=jax.ShapeDtypeStruct((1, s_all), jnp.float32),
        compiler_params=pltpu.CompilerParams(
            dimension_semantics=("arbitrary", "arbitrary"), vmem_limit_bytes=VMEM
        ),
        interpret=interpret,
    )(first, lat, cb, lt)


def _spread_kernel(first_ref, lat_ref, cb_ref, lt_ref, w_ref, out_ref):
    j = pl.program_id(1)
    groups = _lane_groups(jnp.exp(_logits(lat_ref, cb_ref) - lt_ref[:, 0:1]))
    weights = _lane_groups(w_ref[...])
    part = groups[0] * weights[0]
    for g, w in zip(groups[1:], weights[1:]):
        part = part + g * w

    @pl.when(j == 0)
    def _():
        out_ref[...] = part

    @pl.when(j > 0)
    def _():
        out_ref[...] = out_ref[...] + part


def spread_sums(lat, cb, lt, w, first, s_all, interpret=False):
    t_all, d = lat.shape
    tm, tn = min(TM, t_all), min(TN, s_all)
    return pl.pallas_call(
        _spread_kernel,
        grid_spec=pltpu.PrefetchScalarGridSpec(
            num_scalar_prefetch=1,
            grid=(t_all // tm, s_all // tn),
            in_specs=[
                pl.BlockSpec((tm, d), lambda i, j, f: (i, 0)),
                pl.BlockSpec((tn, d), lambda i, j, f: (j + f[0], 0)),
                pl.BlockSpec((tm, 128), lambda i, j, f: (i, 0)),
                pl.BlockSpec((1, tn), lambda i, j, f: (0, j)),
            ],
            out_specs=pl.BlockSpec((tm, 128), lambda i, j, f: (i, 0)),
        ),
        out_shape=jax.ShapeDtypeStruct((t_all, 128), jnp.float32),
        compiler_params=pltpu.CompilerParams(
            dimension_semantics=("arbitrary", "arbitrary"), vmem_limit_bytes=VMEM
        ),
        interpret=interpret,
    )(first, lat, cb, lt, w)


def _grad_kernel(first_ref, lat_ref, cb_ref, lt_ref, rowc_ref, tgt_ref, hw_ref, *refs, tm, tn, carry):
    if carry:
        prev_ref, tok_ref, cbg_ref = refs
    else:
        tok_ref, cbg_ref = refs
    j = pl.program_id(0)
    i = pl.program_id(1)
    logits = _logits(lat_ref, cb_ref)
    probs = jnp.exp(logits - lt_ref[:, 0:1])
    cols = j * tn + lax.broadcasted_iota(jnp.int32, logits.shape, 1)
    hit = (cols == tgt_ref[:, 0:1]).astype(jnp.float32)
    grad = (probs * (rowc_ref[:, 0:1] + hw_ref[...] - 0.5 * logits) - hit).astype(jnp.bfloat16)
    tok = jnp.dot(grad, cb_ref[...], preferred_element_type=jnp.float32)
    cbg = lax.dot_general(
        grad, lat_ref[...], (((0,), (0,)), ((), ())), preferred_element_type=jnp.float32
    )
    rows = pl.ds(pl.multiple_of(i * tm, tm), tm)

    @pl.when(j == 0)
    def _():
        tok_ref[rows, :] = tok

    @pl.when(j > 0)
    def _():
        tok_ref[rows, :] = tok_ref[rows, :] + tok

    @pl.when(i == 0)
    def _():
        cbg_ref[...] = prev_ref[...] + cbg if carry else cbg

    @pl.when(i > 0)
    def _():
        cbg_ref[...] = cbg_ref[...] + cbg


def grads(lat, cb, lt, rowc, tgt, hw, first, s_all, prev=None, interpret=False):
    t_all, d = lat.shape
    tm, tn = min(TM, t_all), min(TN, s_all)
    row = pl.BlockSpec((tm, 128), lambda j, i, f: (i, 0))
    slab_block = pl.BlockSpec((tn, d), lambda j, i, f: (j, 0))
    return pl.pallas_call(
        functools.partial(_grad_kernel, tm=tm, tn=tn, carry=prev is not None),
        grid_spec=pltpu.PrefetchScalarGridSpec(
            num_scalar_prefetch=1,
            grid=(s_all // tn, t_all // tm),
            in_specs=[
                pl.BlockSpec((tm, d), lambda j, i, f: (i, 0)),
                pl.BlockSpec((tn, d), lambda j, i, f: (j + f[0], 0)),
                row,
                row,
                row,
                pl.BlockSpec((1, tn), lambda j, i, f: (0, j)),
            ] + ([] if prev is None else [slab_block]),
            out_specs=[pl.BlockSpec((t_all, d), lambda j, i, f: (0, 0)), slab_block],
        ),
        out_shape=[
            jax.ShapeDtypeStruct((t_all, d), jnp.float32),
            jax.ShapeDtypeStruct((s_all, d), jnp.float32),
        ],
        compiler_params=pltpu.CompilerParams(
            dimension_semantics=("arbitrary", "arbitrary"), vmem_limit_bytes=VMEM
        ),
        input_output_aliases={} if prev is None else {7: 1},
        interpret=interpret,
    )(first, lat, cb, lt, rowc, tgt, hw, *([] if prev is None else [prev]))


def butterfly(values, axis, count, combine):
    step = 1
    while step < count:
        pairs = [(i, i ^ step) for i in range(count)]
        values = combine(values, lax.ppermute(values, axis, pairs))
        step *= 2
    return values


def butterfly_gather(block, axis, count, dim=0):
    index = lax.axis_index(axis)
    step = 1
    while step < count:
        pairs = [(i, i ^ step) for i in range(count)]
        other = lax.ppermute(block, axis, pairs)
        low = (index // step) % 2 == 0
        block = jnp.where(
            low, jnp.concatenate([block, other], dim), jnp.concatenate([other, block], dim)
        )
        step *= 2
    return block


def softmax_merge(a, b):
    top = jnp.maximum(a[0], b[0])
    wa = jnp.exp(a[0] - top)
    wb = jnp.exp(b[0] - top)
    return jnp.stack([top, a[1] * wa + b[1] * wb, a[2] * wa + b[2] * wb])


def lanes(row_values):
    return jnp.broadcast_to(row_values[:, None], (row_values.shape[0], 128))


def is_pow2(n):
    return n & (n - 1) == 0


def rotate(latent, code_vec, cotangent):
    latent_norm = jnp.sqrt(jnp.sum(latent * latent, axis=1, keepdims=True) + norm_eps)
    code_norm = jnp.sqrt(jnp.sum(code_vec * code_vec, axis=1, keepdims=True) + norm_eps)
    latent_dir = latent / latent_norm
    code_dir = code_vec / code_norm
    cosine = jnp.sum(latent_dir * code_dir, axis=1, keepdims=True)
    summed = latent_dir + code_dir
    along = jnp.sum(summed * cotangent, axis=1, keepdims=True)
    facing = jnp.sum(code_dir * cotangent, axis=1, keepdims=True)
    turned = (
        cotangent
        - summed * along / jnp.maximum(1.0 + cosine, cos_floor)
        + 2.0 * latent_dir * facing
    )
    return code_norm / latent_norm * turned


def local(latents, codebook, hard_code, upstream):
    n_dp = lax.axis_size("dp")
    n_code = lax.axis_size("code")
    n_all = n_dp * n_code
    dp_i = lax.axis_index("dp")
    code_i = lax.axis_index("code")
    row_count = latents.shape[0]
    code_count = codebook.shape[0]
    width = latents.shape[1]
    tokens_total = row_count * n_dp
    slab = code_count // n_dp
    owned = row_count // n_code
    all_lat = lax.all_gather(latents, "dp", tiled=True)
    if is_pow2(n_dp):
        all_hard = butterfly_gather(hard_code, "dp", n_dp)
    else:
        all_hard = lax.all_gather(hard_code, "dp", tiled=True)
    first = jnp.reshape(dp_i * (slab // min(TN, slab)), (1,)).astype(jnp.int32)
    offset = code_i * code_count + dp_i * slab

    lane_top, lane_total, lane_moment = row_stats(latents, codebook)
    shard_target = hard_code - code_i * code_count
    holder = ((shard_target >= 0) & (shard_target < code_count))[:, None]
    late_codebook, _ = lax.optimization_barrier((codebook, lane_top))
    picked_vec = jnp.where(
        holder, jnp.take(late_codebook, jnp.clip(shard_target, 0, code_count - 1), axis=0), 0
    ).astype(jnp.bfloat16)
    picked_vec = lax.all_to_all(picked_vec.reshape(n_code, owned, width), "code", 0, 0, tiled=False)
    code_vec = jnp.sum(picked_vec.astype(jnp.float32), axis=0)
    own_lat = lax.dynamic_slice_in_dim(latents, code_i * owned, owned, axis=0).astype(jnp.float32)
    own_up = lax.dynamic_slice_in_dim(upstream, code_i * owned, owned, axis=0).astype(jnp.float32)
    rotated = rotate(own_lat, code_vec, own_up)
    picked_sum = jnp.sum(LOGIT_SCALE * jnp.sum(own_lat * code_vec, axis=1))

    local_top = jnp.max(lane_top, axis=1)
    lane_scale = jnp.exp(lane_top - local_top[:, None])
    stats = jnp.stack([
        local_top, jnp.sum(lane_total * lane_scale, axis=1), jnp.sum(lane_moment * lane_scale, axis=1)
    ])
    if is_pow2(n_code):
        row_top, row_total, moment = butterfly(stats, "code", n_code, softmax_merge)
    else:
        row_top = lax.pmax(stats[0], "code")
        scale = jnp.exp(stats[0] - row_top)
        row_total, moment = lax.psum((stats[1] * scale, stats[2] * scale), "code")
    token_stats = jnp.stack([row_top + jnp.log(row_total), moment / row_total])
    if is_pow2(n_dp):
        token_stats = butterfly_gather(token_stats, "dp", n_dp, dim=1)
    else:
        token_stats = lax.all_gather(token_stats, "dp", axis=1, tiled=True)
    log_total = token_stats[0]
    mean_logit = token_stats[1]
    entropy = log_total - mean_logit
    mean_usage = usage_sums(all_lat, codebook, lanes(log_total), first, slab)[0] / tokens_total
    log_usage = jnp.log(mean_usage + usage_eps)
    weight_term = log_usage + mean_usage / (mean_usage + usage_eps)
    spread_local = jnp.sum(spread_sums(all_lat, codebook, lanes(log_total), weight_term[None, :], first, slab), axis=1)
    extras = jnp.stack([-jnp.sum(mean_usage * log_usage), picked_sum])
    joined = jnp.concatenate([spread_local, extras])
    if is_pow2(n_all):
        joined = butterfly(joined, BOTH, n_all, jnp.add)
    else:
        joined = lax.psum(joined, BOTH)
    spread, usage_entropy, picked_total = joined[:-2], joined[-2], joined[-1]

    row_coef = 1.0 + ENTROPY_WEIGHT * (mean_logit - spread)
    target = (all_hard - offset).astype(jnp.int32)
    chunks = 4 if owned % 4 == 0 and (tokens_total // 4) % min(TM, tokens_total // 4) == 0 else 1
    piece = owned // chunks

    def reorder(x):
        x = x.reshape((n_all, chunks, piece) + x.shape[1:])
        return jnp.swapaxes(x, 0, 1).reshape((chunks, n_all * piece) + x.shape[3:])

    lat_c, lt_c, coef_c, tgt_c = (
        reorder(v) for v in (all_lat, lanes(log_total), lanes(row_coef), lanes(target))
    )
    half_weight = ENTROPY_WEIGHT * weight_term[None, :]
    code_acc = None
    parts = []
    for q in range(chunks):
        token_acc, code_acc = grads(
            lat_c[q], codebook, lt_c[q], coef_c[q], tgt_c[q], half_weight, first, slab, prev=code_acc
        )
        token_acc = (LOGIT_SCALE * token_acc).astype(jnp.bfloat16).reshape(n_all, piece, width)
        token_acc = lax.all_to_all(token_acc, BOTH, 0, 0, tiled=False)
        parts.append(jnp.sum(token_acc.astype(jnp.float32), axis=0))
    token_sum = jnp.concatenate(parts, axis=0)
    codebook_grad = LOGIT_SCALE * code_acc
    token_grad = token_sum + rotated
    loss_terms = jnp.stack([
        (jnp.sum(log_total) - picked_total) / tokens_total,
        jnp.sum(entropy) / tokens_total,
        usage_entropy,
    ])
    return (token_grad, codebook_grad, loss_terms)


def solution(mesh):
    placed = (P("dp", None), P("code", None), P("dp"), P("dp", None))
    return jax.shard_map(
        local,
        mesh=mesh,
        in_specs=placed,
        out_specs=(P(("dp", "code"), None), P(("code", "dp"), None), P()),
        check_vma=False,
    )
```
